256 devices in a mesh: gx: 8 (over z), gy: 32 (over y, x, core).
Axes of the slice: x: 4, y: 4, z: 8, core: 2. Of those that a mesh axis runs over, the one named last changes fastest.
Arguments:
- saved_pops: bfloat16 [4, 19, 128, 16384], P(None, None, 'gx', 'gy'), may hold values from 0.099609375 to 1.8984375
- seed_adjoint: float32 [19, 128, 16384], P(None, 'gx', 'gy'), may hold values from -6 to 6
- solid_label: int32 [128, 16384], P('gx', 'gy'), may hold values 0 or 1
- design_mask: int32 [128, 16384], P('gx', 'gy'), may hold values 0 or 1
- design_field: float32 [128, 16384], P('gx', 'gy'), may hold values from 0 to 1
Outputs:
- adjoint_out: float32 [19, 128, 16384], P(None, 'gx', 'gy')
- sensitivity: float32 [128, 16384], P('gx', 'gy')
The draws below stay inside these ranges and needn't reach their ends.
All inputs are finite; a program needn't handle non-finite values. No bound on the sum of `solid_label` or of `design_mask` on one device may be relied on, other than what follows from the above.
Results may differ from the reference program's by a relative error of at most 0.0003.
Values sent between devices are 32-bit elements; how exact they have to be, the bound alone decides.
No kernel may reach another device: no remote copies, remote signals or barrier semaphores. Data moves between devices by JAX's collectives and lax.ppermute only.
A program may use at most 64 MiB of HBM per device.

```python
import jax
import jax.numpy as jnp
import numpy as np
from jax import lax

CX = 16
NZ = 32
STEPS = 4
NX = 128
NY = 512
N_GX = 8


def set_ends(values, own_key, low, top_value):
    longest = values.shape.index(max(values.shape))
    spots = []
    for shift in (0, 1):
        where = [jax.random.randint(jax.random.fold_in(own_key, axis), (), 0, length) for axis, length in enumerate(values.shape)]
        where[longest] = (where[longest] + shift) % values.shape[longest]
        spots.append(tuple(where))
    return values.at[spots[0]].set(low).at[spots[1]].set(top_value)


def block_levels(rng, shape, pieces, low, top_value):
    loudness = 1.0
    for axis_at, shards_of in pieces:
        heights = jax.random.uniform(jax.random.fold_in(jax.random.fold_in(rng, 6), axis_at), (shards_of,), jnp.float32, low / len(pieces), top_value / len(pieces))
        loudness = loudness * jnp.repeat(jnp.exp(heights), shape[axis_at] // shards_of).reshape((-1,) + (1,) * (len(shape) - 1 - axis_at))
    return loudness


def normal_values(key, extent, spread, bound, cuts=(), held_as=jnp.bfloat16):
    values = spread * jax.random.normal(key, extent, jnp.float32)
    if cuts:
        values = values * block_levels(key, extent, cuts, -0.22, 0.18)
    return jnp.clip(values, -bound, bound).astype(held_as)


def setup_inputs(seed: int = 0) -> dict:
    arg_keys = jax.random.split(jax.random.key(seed), 6)
    saved_pops = jnp.clip(1.0 + 0.18 * jax.random.normal(arg_keys[0], (STEPS, 19, NX, NY * NZ), jnp.float32), 0.099609375, 1.8984375).astype(jnp.bfloat16)
    seed_adjoint = normal_values(arg_keys[1], (19, NX, NY * NZ), 1.0, 6.0, ((1, 8), (2, 32)), jnp.float32)
    solid_label = set_ends((jax.random.randint(arg_keys[2], (NX, NY * NZ), 0, 4) < 1).astype(jnp.int32), jax.random.fold_in(arg_keys[2], 1), 0, 1)
    design_mask = set_ends((jax.random.randint(arg_keys[3], (NX, NY * NZ), 0, 2) < 1).astype(jnp.int32), jax.random.fold_in(arg_keys[3], 1), 0, 1)
    design_field = jnp.clip(1.0 * jax.random.uniform(arg_keys[4], (NX, NY * NZ), jnp.float32) ** block_levels(arg_keys[4], (NX, NY * NZ), ((0, 8), (1, 32)), -0.2, 0.2), 0.0, 1.0)
    return dict(saved_pops=saved_pops, seed_adjoint=seed_adjoint, solid_label=solid_label, design_mask=design_mask, design_field=design_field)


VELOCITIES = np.array([[0, 0, 0], [1, 0, 0], [-1, 0, 0], [0, 1, 0], [0, -1, 0], [0, 0, 1], [0, 0, -1], [1, 1, 0], [1, -1, 0], [-1, 1, 0], [-1, -1, 0], [1, 0, 1], [1, 0, -1], [-1, 0, 1], [-1, 0, -1], [0, 1, 1], [0, 1, -1], [0, -1, 1], [0, -1, -1]])
LATTICE_WEIGHTS = np.array([1.0 / 3.0] + [1.0 / 18.0] * 6 + [1.0 / 36.0] * 12)
OPPOSITE = np.array([0, 2, 1, 4, 3, 6, 5, 10, 9, 8, 7, 14, 13, 12, 11, 18, 17, 16, 15])
OMEGA_BASE = 1.0
OMEGA_SPAN = 0.8
SENS_SCALE = 10.0

def collide(pops, rates, solid):
    density = lax.optimization_barrier(jnp.sum(pops, axis=0))
    velo = jnp.asarray(VELOCITIES, jnp.float32)
    momentum = jnp.tensordot(velo.T, pops, axes=1, precision=lax.Precision.HIGHEST)
    speed = momentum / density
    projected = jnp.tensordot(velo, speed, axes=1, precision=lax.Precision.HIGHEST)
    speed_sq = lax.optimization_barrier(jnp.sum(speed * speed, axis=0))
    weights = jnp.asarray(LATTICE_WEIGHTS, jnp.float32).reshape((19,) + (1,) * (pops.ndim - 1))
    equilibrium = weights * density * (1.0 + 3.0 * projected + 4.5 * projected * projected - 1.5 * speed_sq)
    fluid = pops - rates * (pops - equilibrium)
    bounce = pops[OPPOSITE]
    return jnp.where(solid > 0, bounce, fluid)

def adjoint_block(args):
    pops, pulled, rates, solid = args

    def local(values, rate_values):
        return collide(values, rate_values, solid)
    unused, backward = jax.vjp(local, pops, rates)
    return backward(pulled)

def reference(saved_pops, seed_adjoint, solid_label, design_mask, design_field):
    mask_float = design_mask.astype(jnp.float32)
    rates = OMEGA_BASE + OMEGA_SPAN * design_field * mask_float
    weights = jnp.asarray(LATTICE_WEIGHTS, jnp.float32).reshape(19, 1, 1)
    flat = NY * NZ
    adjoint = seed_adjoint
    sensitivity = jnp.zeros((NX, flat), jnp.float32)

    def blocks(array):
        lead = array.shape[:-2]
        moved = array.reshape(lead + (N_GX, CX, flat))
        return jnp.moveaxis(moved, len(lead), 0)

    def unblock(array):
        lead = array.shape[1:-2]
        moved = jnp.moveaxis(array, 0, len(lead))
        return moved.reshape(lead + (NX, flat))
    for step in reversed(range(STEPS)):
        cube = adjoint.reshape(19, NX, NY, NZ)
        pulled = jnp.stack([jnp.roll(cube[k], (-int(VELOCITIES[k, 0]), -int(VELOCITIES[k, 1]), -int(VELOCITIES[k, 2])), (0, 1, 2)) for k in range(19)])
        pulled = pulled.reshape(19, NX, flat)
        pops = saved_pops[step].astype(jnp.float32) * weights
        new_adj, rate_bar = lax.map(adjoint_block, (blocks(pops), blocks(pulled), blocks(rates), blocks(solid_label)))
        adjoint = unblock(new_adj)
        sensitivity = sensitivity + SENS_SCALE * OMEGA_SPAN * mask_float * unblock(rate_bar)
    return (adjoint, sensitivity)
```

```python
import jax
import jax.numpy as jnp
import numpy as np
from jax import lax
from jax.experimental import pallas as pl
from jax.experimental.pallas import tpu as pltpu
from jax.sharding import PartitionSpec as P

NZ = 32


VELOCITIES = np.array(
    [
        [0, 0, 0],
        [1, 0, 0],
        [-1, 0, 0],
        [0, 1, 0],
        [0, -1, 0],
        [0, 0, 1],
        [0, 0, -1],
        [1, 1, 0],
        [1, -1, 0],
        [-1, 1, 0],
        [-1, -1, 0],
        [1, 0, 1],
        [1, 0, -1],
        [-1, 0, 1],
        [-1, 0, -1],
        [0, 1, 1],
        [0, 1, -1],
        [0, -1, 1],
        [0, -1, -1],
    ]
)
LATTICE_WEIGHTS = np.array([1.0 / 3.0] + [1.0 / 18.0] * 6 + [1.0 / 36.0] * 12)
OPPOSITE = np.array([0, 2, 1, 4, 3, 6, 5, 10, 9, 8, 7, 14, 13, 12, 11, 18, 17, 16, 15])
OMEGA_BASE = 1.0
OMEGA_SPAN = 0.8
SENS_SCALE = 10.0

W32 = [float(np.float32(w)) for w in LATTICE_WEIGHTS]
XP = [i for i in range(19) if VELOCITIES[i, 0] == 1]
XM = [i for i in range(19) if VELOCITIES[i, 0] == -1]
YP = [i for i in range(19) if VELOCITIES[i, 1] == 1]
YM = [i for i in range(19) if VELOCITIES[i, 1] == -1]
LANES = 128


def _build_pulled(adj_ref, rxp, rxm, ryp, rym, rc7, rc8, rc9, rc10, pl_ref):
    _, rows, flat = adj_ref.shape
    tiles = flat // LANES
    row = lax.broadcasted_iota(jnp.int32, (rows, flat), 0)
    rowh = lax.broadcasted_iota(jnp.int32, (rows, LANES), 0)
    lane = lax.broadcasted_iota(jnp.int32, (rows, LANES), 1)
    zl = lane % NZ
    corners = {7: rc7, 8: rc8, 9: rc9, 10: rc10}
    for i in range(19):
        cx, cy, cz = (int(c) for c in VELOCITIES[i])
        v = adj_ref[i]
        if cx == 1:
            j = XP.index(i)
            v = jnp.where(row == rows - 1, rxp[j : j + 1, :], pltpu.roll(v, rows - 1, 0))
        elif cx == -1:
            j = XM.index(i)
            v = jnp.where(row == 0, rxm[j : j + 1, :], pltpu.roll(v, 1, 0))
        pieces = [v[:, LANES * t : LANES * (t + 1)] for t in range(tiles)]
        if cy != 0:
            h = ryp[YP.index(i)] if cy == 1 else rym[YM.index(i)]
            if cx == 1:
                h = jnp.where(rowh == rows - 1, corners[i][...], pltpu.roll(h, rows - 1, 0))
            elif cx == -1:
                h = jnp.where(rowh == 0, corners[i][...], pltpu.roll(h, 1, 0))
            if cy == 1:
                r = [pltpu.roll(p, LANES - NZ, 1) for p in pieces] + [pltpu.roll(h, LANES - NZ, 1)]
                pieces = [jnp.where(lane >= LANES - NZ, r[t + 1], r[t]) for t in range(tiles)]
            else:
                r = [pltpu.roll(h, NZ, 1)] + [pltpu.roll(p, NZ, 1) for p in pieces]
                pieces = [jnp.where(lane < NZ, r[t], r[t + 1]) for t in range(tiles)]
        if cz == 1:
            pieces = [
                jnp.where(zl == NZ - 1, pltpu.roll(p, NZ - 1, 1), pltpu.roll(p, LANES - 1, 1))
                for p in pieces
            ]
        elif cz == -1:
            pieces = [
                jnp.where(zl == 0, pltpu.roll(p, LANES - NZ + 1, 1), pltpu.roll(p, 1, 1))
                for p in pieces
            ]
        for t in range(tiles):
            pl_ref[i, :, LANES * t : LANES * (t + 1)] = pieces[t]


def _collide_vjp(f, g, rate, solid):
    rho = f[0]
    for i in range(1, 19):
        rho = rho + f[i]
    mom = []
    for a in range(3):
        pos = [f[i] for i in range(19) if VELOCITIES[i, a] > 0]
        neg = [f[i] for i in range(19) if VELOCITIES[i, a] < 0]
        acc = pos[0]
        for x in pos[1:]:
            acc = acc + x
        for x in neg:
            acc = acc - x
        mom.append(acc)
    u = [m / rho for m in mom]
    usq = u[0] * u[0] + u[1] * u[1] + u[2] * u[2]
    base = 1.0 - 1.5 * usq
    fluid = solid == 0
    one_minus = 1.0 - rate
    rbar = None
    esum = None
    easum = None
    mb = [None, None, None]
    proj = []
    amp = []
    gf = []
    for i in range(19):
        cvec = [int(c) for c in VELOCITIES[i]]
        p = None
        for a in range(3):
            if cvec[a] == 0:
                continue
            term = u[a] if cvec[a] > 0 else -u[a]
            p = term if p is None else p + term
        if p is None:
            amp_i = base
        else:
            amp_i = base + (3.0 + 4.5 * p) * p
        proj.append(p)
        amp.append(amp_i)
        gi = jnp.where(fluid, g[i], 0.0)
        gf.append(gi)
        feq = W32[i] * rho * amp_i
        t = gi * (feq - f[i])
        rbar = t if rbar is None else rbar + t
        e = (rate * W32[i]) * gi
        esum = e if esum is None else esum + e
        ea = e * amp_i
        easum = ea if easum is None else easum + ea
        if p is not None:
            ep = e * (3.0 + 9.0 * p)
            for a in range(3):
                if cvec[a] == 0:
                    continue
                if mb[a] is None:
                    mb[a] = ep if cvec[a] > 0 else -ep
                else:
                    mb[a] = mb[a] + ep if cvec[a] > 0 else mb[a] - ep
    mb = [mb[a] - 3.0 * u[a] * esum for a in range(3)]
    rhobar = easum - (mb[0] * u[0] + mb[1] * u[1] + mb[2] * u[2])
    out = []
    for i in range(19):
        cvec = [int(c) for c in VELOCITIES[i]]
        val = one_minus * gf[i] + rhobar
        for a in range(3):
            if cvec[a] > 0:
                val = val + mb[a]
            elif cvec[a] < 0:
                val = val - mb[a]
        out.append(jnp.where(fluid, val, g[int(OPPOSITE[i])]))
    return out, rbar


def _write_sends(out_ref, sxm, sxp, sym, syp, s7, s8, s9, s10):
    _, rows, flat = out_ref.shape
    sxm[...] = jnp.zeros(sxm.shape, jnp.float32)
    sxp[...] = jnp.zeros(sxp.shape, jnp.float32)
    for j, i in enumerate(XP):
        sxm[j : j + 1, :] = out_ref[i, 0:1, :]
    for j, i in enumerate(XM):
        sxp[j : j + 1, :] = out_ref[i, rows - 1 : rows, :]
    for j, i in enumerate(YP):
        sym[j] = out_ref[i, :, 0:LANES]
    for j, i in enumerate(YM):
        syp[j] = out_ref[i, :, flat - LANES : flat]
    s7[...] = out_ref[7, 0:1, 0:LANES]
    s8[...] = out_ref[8, 0:1, flat - LANES : flat]
    s9[...] = out_ref[9, rows - 1 : rows, 0:LANES]
    s10[...] = out_ref[10, rows - 1 : rows, flat - LANES : flat]


def _step_kernel(first, last, *refs):
    pops_ref, adj_ref, solid_ref, mask_ref, field_ref = refs[:5]
    halo = refs[5:13]
    k = 13
    if first:
        sens_in = None
    else:
        sens_in = refs[k]
        k += 1
    out_ref, sens_out = refs[k], refs[k + 1]
    sends = refs[k + 2 : k + 10] if not last else None
    pl_ref = refs[-1]
    _build_pulled(adj_ref, *halo, pl_ref)
    _, rows, flat = adj_ref.shape
    for t in range(flat // LANES):
        sl = slice(LANES * t, LANES * (t + 1))
        f = [pops_ref[0, i, :, sl].astype(jnp.float32) * W32[i] for i in range(19)]
        g = [pl_ref[i, :, sl] for i in range(19)]
        mask = mask_ref[:, sl].astype(jnp.float32)
        rate = OMEGA_BASE + OMEGA_SPAN * field_ref[:, sl] * mask
        solid = solid_ref[:, sl]
        new, rbar = _collide_vjp(f, g, rate, solid)
        for i in range(19):
            out_ref[i, :, sl] = new[i]
        contrib = SENS_SCALE * OMEGA_SPAN * mask * jnp.where(solid == 0, rbar, 0.0)
        if first:
            sens_out[:, sl] = contrib
        else:
            sens_out[:, sl] = sens_in[:, sl] + contrib
    if not last:
        _write_sends(out_ref, *sends)


def _pack_kernel(adj_ref, *sends):
    _write_sends(adj_ref, *sends)


def _full(shape):
    nd = len(shape)
    return pl.BlockSpec(shape, lambda i, _n=nd: (0,) * _n)


def _send_shapes(rows, flat):
    return [
        (8, flat),
        (8, flat),
        (len(YP), rows, LANES),
        (len(YM), rows, LANES),
        (1, LANES),
        (1, LANES),
        (1, LANES),
        (1, LANES),
    ]


def _pack(adj):
    _, rows, flat = adj.shape
    shapes = _send_shapes(rows, flat)
    return pl.pallas_call(
        _pack_kernel,
        grid=(1,),
        in_specs=[_full(adj.shape)],
        out_specs=[_full(s) for s in shapes],
        out_shape=[jax.ShapeDtypeStruct(s, jnp.float32) for s in shapes],
    )(adj)


def _step(step, first, last, saved_pops, adj, solid, mask, field, halo, sens):
    _, rows, flat = adj.shape
    shapes = _send_shapes(rows, flat)
    args = [saved_pops, adj, solid, mask, field] + list(halo)
    in_specs = [pl.BlockSpec((1, 19, rows, flat), lambda i, _s=step: (_s, 0, 0, 0))]
    in_specs += [_full(a.shape) for a in args[1:]]
    aliases = {}
    if not first:
        aliases = {len(args): 1}
        args.append(sens)
        in_specs.append(_full(sens.shape))
    out_shapes = [adj.shape, (rows, flat)] + ([] if last else shapes)
    kernel = lambda *refs: _step_kernel(first, last, *refs)
    return pl.pallas_call(
        kernel,
        grid=(1,),
        in_specs=in_specs,
        out_specs=[_full(s) for s in out_shapes],
        out_shape=[jax.ShapeDtypeStruct(s, jnp.float32) for s in out_shapes],
        scratch_shapes=[pltpu.VMEM(adj.shape, jnp.float32)],
        input_output_aliases=aliases,
    )(*args)


def _exchange(sends):
    nx = lax.axis_size("gx")
    ny = lax.axis_size("gy")
    sxm, sxp, sym, syp, s7, s8, s9, s10 = sends

    def shift(n, d):
        return [(i, (i + d) % n) for i in range(n)]

    def diag(dx, dy):
        return [
            (i * ny + j, ((i + dx) % nx) * ny + (j + dy) % ny) for i in range(nx) for j in range(ny)
        ]

    rxp = lax.ppermute(sxm, "gx", shift(nx, -1))
    rxm = lax.ppermute(sxp, "gx", shift(nx, 1))
    ryp = lax.ppermute(sym, "gy", shift(ny, -1))
    rym = lax.ppermute(syp, "gy", shift(ny, 1))
    both = ("gx", "gy")
    rc7 = lax.ppermute(s7, both, diag(-1, -1))
    rc8 = lax.ppermute(s8, both, diag(-1, 1))
    rc9 = lax.ppermute(s9, both, diag(1, -1))
    rc10 = lax.ppermute(s10, both, diag(1, 1))
    return [rxp, rxm, ryp, rym, rc7, rc8, rc9, rc10]


def body(saved_pops, seed_adjoint, solid_label, design_mask, design_field):
    num_steps = saved_pops.shape[0]
    adjoint = seed_adjoint
    sensitivity = None
    halo = _exchange(_pack(adjoint))
    for n, step in enumerate(reversed(range(num_steps))):
        first = n == 0
        last = step == 0
        outs = _step(
            step, first, last, saved_pops, adjoint, solid_label, design_mask, design_field, halo,
            sensitivity,
        )
        adjoint, sensitivity = outs[0], outs[1]
        if not last:
            halo = _exchange(outs[2:])
    return (adjoint, sensitivity)


def solution(mesh):
    in_specs = (
        P(None, None, "gx", "gy"),
        P(None, "gx", "gy"),
        P("gx", "gy"),
        P("gx", "gy"),
        P("gx", "gy"),
    )
    out_specs = (P(None, "gx", "gy"), P("gx", "gy"))
    return jax.shard_map(body, mesh=mesh, in_specs=in_specs, out_specs=out_specs, check_vma=False)
```

```python
import jax
import jax.numpy as jnp
import numpy as np
from jax import lax
from jax.experimental import pallas as pl
from jax.experimental.pallas import tpu as pltpu
from jax.sharding import PartitionSpec as P

NZ = 32


VELOCITIES = np.array(
    [
        [0, 0, 0],
        [1, 0, 0],
        [-1, 0, 0],
        [0, 1, 0],
        [0, -1, 0],
        [0, 0, 1],
        [0, 0, -1],
        [1, 1, 0],
        [1, -1, 0],
        [-1, 1, 0],
        [-1, -1, 0],
        [1, 0, 1],
        [1, 0, -1],
        [-1, 0, 1],
        [-1, 0, -1],
        [0, 1, 1],
        [0, 1, -1],
        [0, -1, 1],
        [0, -1, -1],
    ]
)
LATTICE_WEIGHTS = np.array([1.0 / 3.0] + [1.0 / 18.0] * 6 + [1.0 / 36.0] * 12)
OPPOSITE = np.array([0, 2, 1, 4, 3, 6, 5, 10, 9, 8, 7, 14, 13, 12, 11, 18, 17, 16, 15])
OMEGA_BASE = 1.0
OMEGA_SPAN = 0.8
SENS_SCALE = 10.0

W32 = [float(np.float32(w)) for w in LATTICE_WEIGHTS]
XP = [i for i in range(19) if VELOCITIES[i, 0] == 1]
XM = [i for i in range(19) if VELOCITIES[i, 0] == -1]
YP = [i for i in range(19) if VELOCITIES[i, 1] == 1]
YM = [i for i in range(19) if VELOCITIES[i, 1] == -1]
LANES = 128


def _build_pulled(adj_ref, rxp, rxm, ryp, rym, f7, f8, f9, f10, pl_ref):
    _, rows, flat = adj_ref.shape
    tiles = flat // LANES
    row = lax.broadcasted_iota(jnp.int32, (rows, flat), 0)
    rowh = lax.broadcasted_iota(jnp.int32, (rows, LANES), 0)
    lane = lax.broadcasted_iota(jnp.int32, (rows, LANES), 1)
    zl = lane % NZ
    flat_end = flat - LANES
    corners = {
        7: lambda: f7[XP.index(7) : XP.index(7) + 1, 0:LANES],
        8: lambda: f8[XP.index(8) : XP.index(8) + 1, flat_end:flat],
        9: lambda: f9[XM.index(9) : XM.index(9) + 1, 0:LANES],
        10: lambda: f10[XM.index(10) : XM.index(10) + 1, flat_end:flat],
    }
    for i in range(19):
        cx, cy, cz = (int(c) for c in VELOCITIES[i])
        v = adj_ref[i]
        if cx == 1:
            j = XP.index(i)
            v = jnp.where(row == rows - 1, rxp[j : j + 1, :], pltpu.roll(v, rows - 1, 0))
        elif cx == -1:
            j = XM.index(i)
            v = jnp.where(row == 0, rxm[j : j + 1, :], pltpu.roll(v, 1, 0))
        pieces = [v[:, LANES * t : LANES * (t + 1)] for t in range(tiles)]
        if cy != 0:
            h = ryp[YP.index(i)] if cy == 1 else rym[YM.index(i)]
            if cx == 1:
                h = jnp.where(rowh == rows - 1, corners[i](), pltpu.roll(h, rows - 1, 0))
            elif cx == -1:
                h = jnp.where(rowh == 0, corners[i](), pltpu.roll(h, 1, 0))
            if cy == 1:
                r = [pltpu.roll(p, LANES - NZ, 1) for p in pieces] + [pltpu.roll(h, LANES - NZ, 1)]
                pieces = [jnp.where(lane >= LANES - NZ, r[t + 1], r[t]) for t in range(tiles)]
            else:
                r = [pltpu.roll(h, NZ, 1)] + [pltpu.roll(p, NZ, 1) for p in pieces]
                pieces = [jnp.where(lane < NZ, r[t], r[t + 1]) for t in range(tiles)]
        if cz == 1:
            pieces = [
                jnp.where(zl == NZ - 1, pltpu.roll(p, NZ - 1, 1), pltpu.roll(p, LANES - 1, 1))
                for p in pieces
            ]
        elif cz == -1:
            pieces = [
                jnp.where(zl == 0, pltpu.roll(p, LANES - NZ + 1, 1), pltpu.roll(p, 1, 1))
                for p in pieces
            ]
        for t in range(tiles):
            pl_ref[i, :, LANES * t : LANES * (t + 1)] = pieces[t]


def _collide_vjp(f, g, rate, solid):
    rho = f[0]
    for i in range(1, 19):
        rho = rho + f[i]
    mom = []
    for a in range(3):
        pos = [f[i] for i in range(19) if VELOCITIES[i, a] > 0]
        neg = [f[i] for i in range(19) if VELOCITIES[i, a] < 0]
        acc = pos[0]
        for x in pos[1:]:
            acc = acc + x
        for x in neg:
            acc = acc - x
        mom.append(acc)
    u = [m / rho for m in mom]
    usq = u[0] * u[0] + u[1] * u[1] + u[2] * u[2]
    base = 1.0 - 1.5 * usq
    fluid = solid == 0
    one_minus = 1.0 - rate
    rbar = None
    esum = None
    easum = None
    mb = [None, None, None]
    proj = []
    amp = []
    gf = []
    for i in range(19):
        cvec = [int(c) for c in VELOCITIES[i]]
        p = None
        for a in range(3):
            if cvec[a] == 0:
                continue
            term = u[a] if cvec[a] > 0 else -u[a]
            p = term if p is None else p + term
        if p is None:
            amp_i = base
        else:
            amp_i = base + (3.0 + 4.5 * p) * p
        proj.append(p)
        amp.append(amp_i)
        gi = jnp.where(fluid, g[i], 0.0)
        gf.append(gi)
        feq = W32[i] * rho * amp_i
        t = gi * (feq - f[i])
        rbar = t if rbar is None else rbar + t
        e = (rate * W32[i]) * gi
        esum = e if esum is None else esum + e
        ea = e * amp_i
        easum = ea if easum is None else easum + ea
        if p is not None:
            ep = e * (3.0 + 9.0 * p)
            for a in range(3):
                if cvec[a] == 0:
                    continue
                if mb[a] is None:
                    mb[a] = ep if cvec[a] > 0 else -ep
                else:
                    mb[a] = mb[a] + ep if cvec[a] > 0 else mb[a] - ep
    mb = [mb[a] - 3.0 * u[a] * esum for a in range(3)]
    rhobar = easum - (mb[0] * u[0] + mb[1] * u[1] + mb[2] * u[2])
    out = []
    for i in range(19):
        cvec = [int(c) for c in VELOCITIES[i]]
        val = one_minus * gf[i] + rhobar
        for a in range(3):
            if cvec[a] > 0:
                val = val + mb[a]
            elif cvec[a] < 0:
                val = val - mb[a]
        out.append(jnp.where(fluid, val, g[int(OPPOSITE[i])]))
    return out, rbar


def _write_sends(out_ref, sxm, sxp, sym, syp):
    _, rows, flat = out_ref.shape
    sxm[...] = jnp.zeros(sxm.shape, jnp.float32)
    sxp[...] = jnp.zeros(sxp.shape, jnp.float32)
    for j, i in enumerate(XP):
        sxm[j : j + 1, :] = out_ref[i, 0:1, :]
    for j, i in enumerate(XM):
        sxp[j : j + 1, :] = out_ref[i, rows - 1 : rows, :]
    for j, i in enumerate(YP):
        sym[j] = out_ref[i, :, 0:LANES]
    for j, i in enumerate(YM):
        syp[j] = out_ref[i, :, flat - LANES : flat]


def _step_kernel(first, last, *refs):
    pops_ref, adj_ref, solid_ref, mask_ref, field_ref = refs[:5]
    halo = refs[5:13]
    k = 13
    if first:
        sens_in = None
    else:
        sens_in = refs[k]
        k += 1
    out_ref, sens_out = refs[k], refs[k + 1]
    sends = refs[k + 2 : k + 6] if not last else None
    pl_ref = refs[-1]
    _build_pulled(adj_ref, *halo, pl_ref)
    _, rows, flat = adj_ref.shape
    for t in range(flat // LANES):
        sl = slice(LANES * t, LANES * (t + 1))
        f = [pops_ref[0, i, :, sl].astype(jnp.float32) * W32[i] for i in range(19)]
        g = [pl_ref[i, :, sl] for i in range(19)]
        mask = mask_ref[:, sl].astype(jnp.float32)
        rate = OMEGA_BASE + OMEGA_SPAN * field_ref[:, sl] * mask
        solid = solid_ref[:, sl]
        new, rbar = _collide_vjp(f, g, rate, solid)
        for i in range(19):
            out_ref[i, :, sl] = new[i]
        contrib = SENS_SCALE * OMEGA_SPAN * mask * jnp.where(solid == 0, rbar, 0.0)
        if first:
            sens_out[:, sl] = contrib
        else:
            sens_out[:, sl] = sens_in[:, sl] + contrib
    if not last:
        _write_sends(out_ref, *sends)


def _pack_kernel(adj_ref, *sends):
    _write_sends(adj_ref, *sends)


def _full(shape):
    nd = len(shape)
    return pl.BlockSpec(shape, lambda i, _n=nd: (0,) * _n)


def _send_shapes(rows, flat):
    return [(8, flat), (8, flat), (len(YP), rows, LANES), (len(YM), rows, LANES)]


def _pack(adj):
    _, rows, flat = adj.shape
    shapes = _send_shapes(rows, flat)
    return pl.pallas_call(
        _pack_kernel,
        grid=(1,),
        in_specs=[_full(adj.shape)],
        out_specs=[_full(s) for s in shapes],
        out_shape=[jax.ShapeDtypeStruct(s, jnp.float32) for s in shapes],
    )(adj)


def _step(step, first, last, saved_pops, adj, solid, mask, field, halo, sens):
    _, rows, flat = adj.shape
    shapes = _send_shapes(rows, flat)
    args = [saved_pops, adj, solid, mask, field] + list(halo)
    in_specs = [pl.BlockSpec((1, 19, rows, flat), lambda i, _s=step: (_s, 0, 0, 0))]
    in_specs += [_full(a.shape) for a in args[1:]]
    aliases = {}
    if not first:
        aliases = {len(args): 1}
        args.append(sens)
        in_specs.append(_full(sens.shape))
    out_shapes = [adj.shape, (rows, flat)] + ([] if last else shapes)
    kernel = lambda *refs: _step_kernel(first, last, *refs)
    return pl.pallas_call(
        kernel,
        grid=(1,),
        in_specs=in_specs,
        out_specs=[_full(s) for s in out_shapes],
        out_shape=[jax.ShapeDtypeStruct(s, jnp.float32) for s in out_shapes],
        scratch_shapes=[pltpu.VMEM(adj.shape, jnp.float32)],
        input_output_aliases=aliases,
    )(*args)


def _exchange(sends):
    nx = lax.axis_size("gx")
    ny = lax.axis_size("gy")
    sxm, sxp, sym, syp = sends

    def shift(n, d):
        return [(i, (i + d) % n) for i in range(n)]

    rxp = lax.ppermute(sxm, "gx", shift(nx, -1))
    rxm = lax.ppermute(sxp, "gx", shift(nx, 1))
    ryp = lax.ppermute(sym, "gy", shift(ny, -1))
    rym = lax.ppermute(syp, "gy", shift(ny, 1))
    f7 = lax.ppermute(rxp, "gy", shift(ny, -1))
    f8 = lax.ppermute(rxp, "gy", shift(ny, 1))
    f9 = lax.ppermute(rxm, "gy", shift(ny, -1))
    f10 = lax.ppermute(rxm, "gy", shift(ny, 1))
    return [rxp, rxm, ryp, rym, f7, f8, f9, f10]


def body(saved_pops, seed_adjoint, solid_label, design_mask, design_field):
    num_steps = saved_pops.shape[0]
    adjoint = seed_adjoint
    sensitivity = None
    halo = _exchange(_pack(adjoint))
    for n, step in enumerate(reversed(range(num_steps))):
        first = n == 0
        last = step == 0
        outs = _step(
            step, first, last, saved_pops, adjoint, solid_label, design_mask, design_field, halo,
            sensitivity,
        )
        adjoint, sensitivity = outs[0], outs[1]
        if not last:
            halo = _exchange(outs[2:])
    return (adjoint, sensitivity)


def solution(mesh):
    in_specs = (
        P(None, None, "gx", "gy"),
        P(None, "gx", "gy"),
        P("gx", "gy"),
        P("gx", "gy"),
        P("gx", "gy"),
    )
    out_specs = (P(None, "gx", "gy"), P("gx", "gy"))
    return jax.shard_map(body, mesh=mesh, in_specs=in_specs, out_specs=out_specs, check_vma=False)
```

```python
import jax
import jax.numpy as jnp
import numpy as np
from jax import lax
from jax.experimental import pallas as pl
from jax.experimental.pallas import tpu as pltpu
from jax.sharding import PartitionSpec as P

NZ = 32


VELOCITIES = np.array(
    [
        [0, 0, 0],
        [1, 0, 0],
        [-1, 0, 0],
        [0, 1, 0],
        [0, -1, 0],
        [0, 0, 1],
        [0, 0, -1],
        [1, 1, 0],
        [1, -1, 0],
        [-1, 1, 0],
        [-1, -1, 0],
        [1, 0, 1],
        [1, 0, -1],
        [-1, 0, 1],
        [-1, 0, -1],
        [0, 1, 1],
        [0, 1, -1],
        [0, -1, 1],
        [0, -1, -1],
    ]
)
LATTICE_WEIGHTS = np.array([1.0 / 3.0] + [1.0 / 18.0] * 6 + [1.0 / 36.0] * 12)
OPPOSITE = np.array([0, 2, 1, 4, 3, 6, 5, 10, 9, 8, 7, 14, 13, 12, 11, 18, 17, 16, 15])
OMEGA_BASE = 1.0
OMEGA_SPAN = 0.8
SENS_SCALE = 10.0

W32 = [float(np.float32(w)) for w in LATTICE_WEIGHTS]
XP = [i for i in range(19) if VELOCITIES[i, 0] == 1]
XM = [i for i in range(19) if VELOCITIES[i, 0] == -1]
YP = [i for i in range(19) if VELOCITIES[i, 1] == 1]
YM = [i for i in range(19) if VELOCITIES[i, 1] == -1]
LANES = 128


def _collide_vjp(f, g, rate, solid):
    rho = f[0]
    for i in range(1, 19):
        rho = rho + f[i]
    mom = []
    for a in range(3):
        pos = [f[i] for i in range(19) if VELOCITIES[i, a] > 0]
        neg = [f[i] for i in range(19) if VELOCITIES[i, a] < 0]
        acc = pos[0]
        for x in pos[1:]:
            acc = acc + x
        for x in neg:
            acc = acc - x
        mom.append(acc)
    u = [m / rho for m in mom]
    usq = u[0] * u[0] + u[1] * u[1] + u[2] * u[2]
    base = 1.0 - 1.5 * usq
    fluid = solid == 0
    one_minus = 1.0 - rate
    rbar = None
    esum = None
    easum = None
    mb = [None, None, None]
    proj = []
    amp = []
    gf = []
    for i in range(19):
        cvec = [int(c) for c in VELOCITIES[i]]
        p = None
        for a in range(3):
            if cvec[a] == 0:
                continue
            term = u[a] if cvec[a] > 0 else -u[a]
            p = term if p is None else p + term
        if p is None:
            amp_i = base
        else:
            amp_i = base + (3.0 + 4.5 * p) * p
        proj.append(p)
        amp.append(amp_i)
        gi = jnp.where(fluid, g[i], 0.0)
        gf.append(gi)
        feq = W32[i] * rho * amp_i
        t = gi * (feq - f[i])
        rbar = t if rbar is None else rbar + t
        e = (rate * W32[i]) * gi
        esum = e if esum is None else esum + e
        ea = e * amp_i
        easum = ea if easum is None else easum + ea
        if p is not None:
            ep = e * (3.0 + 9.0 * p)
            for a in range(3):
                if cvec[a] == 0:
                    continue
                if mb[a] is None:
                    mb[a] = ep if cvec[a] > 0 else -ep
                else:
                    mb[a] = mb[a] + ep if cvec[a] > 0 else mb[a] - ep
    mb = [mb[a] - 3.0 * u[a] * esum for a in range(3)]
    rhobar = easum - (mb[0] * u[0] + mb[1] * u[1] + mb[2] * u[2])
    out = []
    for i in range(19):
        cvec = [int(c) for c in VELOCITIES[i]]
        val = one_minus * gf[i] + rhobar
        for a in range(3):
            if cvec[a] > 0:
                val = val + mb[a]
            elif cvec[a] < 0:
                val = val - mb[a]
        out.append(jnp.where(fluid, val, g[int(OPPOSITE[i])]))
    return out, rbar


DEPTH = 4


def _pull_all(a_ref, p_ref):
    _, rows, flat = a_ref.shape
    zl = lax.broadcasted_iota(jnp.int32, (rows, flat), 1) % NZ
    for i in range(19):
        cx, cy, cz = (int(c) for c in VELOCITIES[i])
        v = a_ref[i]
        if cx != 0:
            v = pltpu.roll(v, (rows - cx) % rows, 0)
        if cy != 0:
            v = pltpu.roll(v, (flat - cy * NZ) % flat, 1)
        if cz == 1:
            v = jnp.where(zl == NZ - 1, pltpu.roll(v, NZ - 1, 1), pltpu.roll(v, flat - 1, 1))
        elif cz == -1:
            v = jnp.where(zl == 0, pltpu.roll(v, flat - NZ + 1, 1), pltpu.roll(v, 1, 1))
        p_ref[i] = v


def _fill_ext(dst, own, hxp, hxm, hyp, hym, rows, flat):
    dst[0:rows, 0:flat] = own
    dst[rows : rows + DEPTH, 0:flat] = hxp
    dst[rows + DEPTH : rows + 2 * DEPTH, 0:flat] = hxm
    dst[:, flat : flat + DEPTH * NZ] = hyp
    dst[:, flat + DEPTH * NZ : flat + 2 * DEPTH * NZ] = hym


def _fused_kernel(pops_ref, seed_ref, solid_ref, mask_ref, field_ref, hxp, hxm, hyp, hym,
                  adj_out, sens_out, a_ref, p_ref, f_ref, rate_ref, solid_ext):
    steps = pops_ref.shape[0]
    _, rows, flat = seed_ref.shape
    erows, eflat = a_ref.shape[1], a_ref.shape[2]
    nfield = hxp.shape[0]
    mask_all = mask_ref[...].astype(jnp.float32)
    rate_own = OMEGA_BASE + OMEGA_SPAN * field_ref[...] * mask_all
    _fill_ext(rate_ref, rate_own, hxp[nfield - 2], hxm[nfield - 2], hyp[nfield - 2],
              hym[nfield - 2], rows, flat)
    _fill_ext(solid_ext, solid_ref[...].astype(jnp.float32), hxp[nfield - 1], hxm[nfield - 1],
              hyp[nfield - 1], hym[nfield - 1], rows, flat)
    for i in range(19):
        _fill_ext(a_ref.at[i], seed_ref[i], hxp[i], hxm[i], hyp[i], hym[i], rows, flat)
    sens_out[...] = jnp.zeros(sens_out.shape, jnp.float32)
    row_tiles = rows // 8
    lane_tiles = flat // LANES
    ext_lane_tiles = eflat // LANES
    n_own = row_tiles * lane_tiles
    n_halo_rows = (erows - rows) // 8 * lane_tiles
    n_halo = n_halo_rows + (erows // 8) * (ext_lane_tiles - lane_tiles)

    def chunk(r0, l0, write_ref, own):
        rs = pl.ds(r0, 8)
        ls = pl.ds(l0, LANES)
        f = [f_ref[i, rs, ls] for i in range(19)]
        g = [p_ref[i, rs, ls] for i in range(19)]
        solid = solid_ext[rs, ls]
        solid_i = jnp.where(solid > 0.5, 1, 0)
        new, rbar = _collide_vjp(f, g, rate_ref[rs, ls], solid_i)
        for i in range(19):
            write_ref[i, rs, ls] = new[i]
        if own:
            mask = mask_ref[rs, ls].astype(jnp.float32)
            contrib = SENS_SCALE * OMEGA_SPAN * mask * jnp.where(solid_i == 0, rbar, 0.0)
            sens_out[rs, ls] = sens_out[rs, ls] + contrib

    for n, step in enumerate(reversed(range(steps))):
        last = step == 0
        for i in range(19):
            own = pops_ref[step, i].astype(jnp.float32) * W32[i]
            if last:
                f_ref[i, 0:rows, 0:flat] = own
            else:
                k = 19 + 19 * (steps - 1 - step) + i
                _fill_ext(f_ref.at[i], own, hxp[k] * W32[i], hxm[k] * W32[i], hyp[k] * W32[i],
                          hym[k] * W32[i], rows, flat)
        _pull_all(a_ref, p_ref)
        write_ref = adj_out if last else a_ref

        def own_body(c, carry, write_ref=write_ref):
            r0 = pl.multiple_of((c // lane_tiles) * 8, 8)
            l0 = pl.multiple_of((c % lane_tiles) * LANES, LANES)
            chunk(r0, l0, write_ref, True)
            return carry

        lax.fori_loop(0, n_own, own_body, 0)
        if not last:

            def halo_body(c, carry):
                c2 = c - n_halo_rows
                ext_w = ext_lane_tiles - lane_tiles
                r = jnp.where(c < n_halo_rows, rows // 8 + c // lane_tiles, c2 // ext_w)
                t = jnp.where(c < n_halo_rows, c % lane_tiles, lane_tiles + c2 % ext_w)
                chunk(pl.multiple_of(r * 8, 8), pl.multiple_of(t * LANES, LANES), a_ref, False)
                return carry

            lax.fori_loop(0, n_halo, halo_body, 0)


def _messages(saved_pops, seed, solid, mask, field):
    steps = saved_pops.shape[0]
    rate = OMEGA_BASE + OMEGA_SPAN * field * mask.astype(jnp.float32)
    parts = [seed] + [saved_pops[s].astype(jnp.float32) for s in reversed(range(1, steps))]
    parts += [rate[None], solid.astype(jnp.float32)[None]]
    return jnp.concatenate(parts, axis=0)


def _shift(n, d):
    return [(i, (i + d) % n) for i in range(n)]


def body(saved_pops, seed_adjoint, solid_label, design_mask, design_field):
    nx = lax.axis_size("gx")
    ny = lax.axis_size("gy")
    _, rows, flat = seed_adjoint.shape
    yw = DEPTH * NZ
    fields = _messages(saved_pops, seed_adjoint, solid_label, design_mask, design_field)
    hxp = lax.ppermute(fields[:, 0:DEPTH, :], "gx", _shift(nx, -1))
    hxm = lax.ppermute(fields[:, rows - DEPTH : rows, :], "gx", _shift(nx, 1))
    col_lo = jnp.concatenate([fields[:, :, 0:yw], hxp[:, :, 0:yw], hxm[:, :, 0:yw]], axis=1)
    col_hi = jnp.concatenate(
        [fields[:, :, flat - yw : flat], hxp[:, :, flat - yw : flat], hxm[:, :, flat - yw : flat]],
        axis=1,
    )
    hyp = lax.ppermute(col_lo, "gy", _shift(ny, -1))
    hym = lax.ppermute(col_hi, "gy", _shift(ny, 1))
    erows = rows + 2 * DEPTH
    eflat = flat + 2 * yw
    ext = (19, erows, eflat)
    args = [saved_pops, seed_adjoint, solid_label, design_mask, design_field, hxp, hxm, hyp, hym]

    def full(shape):
        nd = len(shape)
        return pl.BlockSpec(shape, lambda i, _n=nd: (0,) * _n)

    adjoint, sensitivity = pl.pallas_call(
        _fused_kernel,
        grid=(1,),
        in_specs=[full(a.shape) for a in args],
        out_specs=[full(seed_adjoint.shape), full((rows, flat))],
        out_shape=[
            jax.ShapeDtypeStruct(seed_adjoint.shape, jnp.float32),
            jax.ShapeDtypeStruct((rows, flat), jnp.float32),
        ],
        scratch_shapes=[
            pltpu.VMEM(ext, jnp.float32),
            pltpu.VMEM(ext, jnp.float32),
            pltpu.VMEM(ext, jnp.float32),
            pltpu.VMEM((erows, eflat), jnp.float32),
            pltpu.VMEM((erows, eflat), jnp.float32),
        ],
    )(*args)
    return (adjoint, sensitivity)


def solution(mesh):
    in_specs = (
        P(None, None, "gx", "gy"),
        P(None, "gx", "gy"),
        P("gx", "gy"),
        P("gx", "gy"),
        P("gx", "gy"),
    )
    out_specs = (P(None, "gx", "gy"), P("gx", "gy"))
    return jax.shard_map(body, mesh=mesh, in_specs=in_specs, out_specs=out_specs, check_vma=False)
```

```python
import jax
import jax.numpy as jnp
import numpy as np
from jax import lax
from jax.experimental import pallas as pl
from jax.experimental.pallas import tpu as pltpu
from jax.sharding import PartitionSpec as P

NZ = 32


VELOCITIES = np.array(
    [
        [0, 0, 0],
        [1, 0, 0],
        [-1, 0, 0],
        [0, 1, 0],
        [0, -1, 0],
        [0, 0, 1],
        [0, 0, -1],
        [1, 1, 0],
        [1, -1, 0],
        [-1, 1, 0],
        [-1, -1, 0],
        [1, 0, 1],
        [1, 0, -1],
        [-1, 0, 1],
        [-1, 0, -1],
        [0, 1, 1],
        [0, 1, -1],
        [0, -1, 1],
        [0, -1, -1],
    ]
)
LATTICE_WEIGHTS = np.array([1.0 / 3.0] + [1.0 / 18.0] * 6 + [1.0 / 36.0] * 12)
OPPOSITE = np.array([0, 2, 1, 4, 3, 6, 5, 10, 9, 8, 7, 14, 13, 12, 11, 18, 17, 16, 15])
OMEGA_BASE = 1.0
OMEGA_SPAN = 0.8
SENS_SCALE = 10.0

W32 = [float(np.float32(w)) for w in LATTICE_WEIGHTS]
XP = [i for i in range(19) if VELOCITIES[i, 0] == 1]
XM = [i for i in range(19) if VELOCITIES[i, 0] == -1]
YP = [i for i in range(19) if VELOCITIES[i, 1] == 1]
YM = [i for i in range(19) if VELOCITIES[i, 1] == -1]
LANES = 128


def _collide_vjp(f, g, rate, solid):
    rho = f[0]
    for i in range(1, 19):
        rho = rho + f[i]
    mom = []
    for a in range(3):
        pos = [f[i] for i in range(19) if VELOCITIES[i, a] > 0]
        neg = [f[i] for i in range(19) if VELOCITIES[i, a] < 0]
        acc = pos[0]
        for x in pos[1:]:
            acc = acc + x
        for x in neg:
            acc = acc - x
        mom.append(acc)
    u = [m / rho for m in mom]
    usq = u[0] * u[0] + u[1] * u[1] + u[2] * u[2]
    base = 1.0 - 1.5 * usq
    fluid = solid == 0
    one_minus = 1.0 - rate
    rbar = None
    esum = None
    easum = None
    mb = [None, None, None]
    proj = []
    amp = []
    gf = []
    for i in range(19):
        cvec = [int(c) for c in VELOCITIES[i]]
        p = None
        for a in range(3):
            if cvec[a] == 0:
                continue
            term = u[a] if cvec[a] > 0 else -u[a]
            p = term if p is None else p + term
        if p is None:
            amp_i = base
        else:
            amp_i = base + (3.0 + 4.5 * p) * p
        proj.append(p)
        amp.append(amp_i)
        gi = jnp.where(fluid, g[i], 0.0)
        gf.append(gi)
        feq = W32[i] * rho * amp_i
        t = gi * (feq - f[i])
        rbar = t if rbar is None else rbar + t
        e = (rate * W32[i]) * gi
        esum = e if esum is None else esum + e
        ea = e * amp_i
        easum = ea if easum is None else easum + ea
        if p is not None:
            ep = e * (3.0 + 9.0 * p)
            for a in range(3):
                if cvec[a] == 0:
                    continue
                if mb[a] is None:
                    mb[a] = ep if cvec[a] > 0 else -ep
                else:
                    mb[a] = mb[a] + ep if cvec[a] > 0 else mb[a] - ep
    mb = [mb[a] - 3.0 * u[a] * esum for a in range(3)]
    rhobar = easum - (mb[0] * u[0] + mb[1] * u[1] + mb[2] * u[2])
    out = []
    for i in range(19):
        cvec = [int(c) for c in VELOCITIES[i]]
        val = one_minus * gf[i] + rhobar
        for a in range(3):
            if cvec[a] > 0:
                val = val + mb[a]
            elif cvec[a] < 0:
                val = val - mb[a]
        out.append(jnp.where(fluid, val, g[int(OPPOSITE[i])]))
    return out, rbar


DEPTH = 4


def _pull_all(a_ref, p_ref):
    _, rows, flat = a_ref.shape
    zl = lax.broadcasted_iota(jnp.int32, (rows, flat), 1) % NZ
    for i in range(19):
        cx, cy, cz = (int(c) for c in VELOCITIES[i])
        v = a_ref[i]
        if cx != 0:
            v = pltpu.roll(v, (rows - cx) % rows, 0)
        if cy != 0:
            v = pltpu.roll(v, (flat - cy * NZ) % flat, 1)
        if cz == 1:
            v = jnp.where(zl == NZ - 1, pltpu.roll(v, NZ - 1, 1), pltpu.roll(v, flat - 1, 1))
        elif cz == -1:
            v = jnp.where(zl == 0, pltpu.roll(v, flat - NZ + 1, 1), pltpu.roll(v, 1, 1))
        p_ref[i] = v


def _fill_ext(dst, own, hxp, hxm, hyp, hym, cp, cm, rows, flat):
    yw = DEPTH * NZ
    dst[0:rows, 0:flat] = own
    dst[rows : rows + DEPTH, 0:flat] = hxp
    dst[rows + DEPTH : rows + 2 * DEPTH, 0:flat] = hxm
    dst[0:rows, flat : flat + yw] = hyp
    dst[rows : rows + 2 * DEPTH, flat : flat + yw] = cp
    dst[0:rows, flat + yw : flat + 2 * yw] = hym
    dst[rows : rows + 2 * DEPTH, flat + yw : flat + 2 * yw] = cm


def _fused_kernel(pops_ref, seed_ref, solid_ref, mask_ref, field_ref, hxp, hxm, hyp, hym, cp, cm,
                  adj_out, sens_out, a_ref, p_ref, f_ref, rate_ref, solid_ext):
    steps = pops_ref.shape[0]
    _, rows, flat = seed_ref.shape
    erows, eflat = a_ref.shape[1], a_ref.shape[2]
    nfield = hxp.shape[0]
    mask_all = mask_ref[...].astype(jnp.float32)
    rate_own = OMEGA_BASE + OMEGA_SPAN * field_ref[...] * mask_all
    halo = lambda k, scale=None: [
        h[k] if scale is None else h[k] * scale for h in (hxp, hxm, hyp, hym, cp, cm)
    ]
    _fill_ext(rate_ref, rate_own, *halo(nfield - 2), rows, flat)
    _fill_ext(solid_ext, solid_ref[...].astype(jnp.float32), *halo(nfield - 1), rows, flat)
    for i in range(19):
        _fill_ext(a_ref.at[i], seed_ref[i], *halo(i), rows, flat)
    sens_out[...] = jnp.zeros(sens_out.shape, jnp.float32)
    row_tiles = rows // 8
    lane_tiles = flat // LANES
    ext_lane_tiles = eflat // LANES
    n_own = row_tiles * lane_tiles
    n_halo_rows = (erows - rows) // 8 * lane_tiles
    n_halo = n_halo_rows + (erows // 8) * (ext_lane_tiles - lane_tiles)

    def chunk(r0, l0, write_ref, own):
        rs = pl.ds(r0, 8)
        ls = pl.ds(l0, LANES)
        f = [f_ref[i, rs, ls] for i in range(19)]
        g = [p_ref[i, rs, ls] for i in range(19)]
        solid = solid_ext[rs, ls]
        solid_i = jnp.where(solid > 0.5, 1, 0)
        new, rbar = _collide_vjp(f, g, rate_ref[rs, ls], solid_i)
        for i in range(19):
            write_ref[i, rs, ls] = new[i]
        if own:
            mask = mask_ref[rs, ls].astype(jnp.float32)
            contrib = SENS_SCALE * OMEGA_SPAN * mask * jnp.where(solid_i == 0, rbar, 0.0)
            sens_out[rs, ls] = sens_out[rs, ls] + contrib

    for n, step in enumerate(reversed(range(steps))):
        last = step == 0
        for i in range(19):
            own = pops_ref[step, i].astype(jnp.float32) * W32[i]
            if last:
                f_ref[i, 0:rows, 0:flat] = own
            else:
                k = 19 + 19 * (steps - 1 - step) + i
                _fill_ext(f_ref.at[i], own, *halo(k, W32[i]), rows, flat)
        _pull_all(a_ref, p_ref)
        write_ref = adj_out if last else a_ref

        def own_body(c, carry, write_ref=write_ref):
            r0 = pl.multiple_of((c // lane_tiles) * 8, 8)
            l0 = pl.multiple_of((c % lane_tiles) * LANES, LANES)
            chunk(r0, l0, write_ref, True)
            return carry

        lax.fori_loop(0, n_own, own_body, 0)
        if not last:

            def halo_body(c, carry):
                c2 = c - n_halo_rows
                ext_w = ext_lane_tiles - lane_tiles
                r = jnp.where(c < n_halo_rows, rows // 8 + c // lane_tiles, c2 // ext_w)
                t = jnp.where(c < n_halo_rows, c % lane_tiles, lane_tiles + c2 % ext_w)
                chunk(pl.multiple_of(r * 8, 8), pl.multiple_of(t * LANES, LANES), a_ref, False)
                return carry

            lax.fori_loop(0, n_halo, halo_body, 0)


def _message(saved_pops, seed, solid, mask, field, rs, ls):
    steps = saved_pops.shape[0]
    rate = OMEGA_BASE + OMEGA_SPAN * field[rs, ls] * mask[rs, ls].astype(jnp.float32)
    parts = [seed[:, rs, ls]]
    parts += [saved_pops[s][:, rs, ls].astype(jnp.float32) for s in reversed(range(1, steps))]
    parts += [rate[None], solid[rs, ls].astype(jnp.float32)[None]]
    return jnp.concatenate(parts, axis=0)


def _shift(n, d):
    return [(i, (i + d) % n) for i in range(n)]


def body(saved_pops, seed_adjoint, solid_label, design_mask, design_field):
    nx = lax.axis_size("gx")
    ny = lax.axis_size("gy")
    _, rows, flat = seed_adjoint.shape
    yw = DEPTH * NZ
    ins = (saved_pops, seed_adjoint, solid_label, design_mask, design_field)
    full_r, full_l = slice(0, rows), slice(0, flat)
    lo_l, hi_l = slice(0, yw), slice(flat - yw, flat)
    hxp = lax.ppermute(_message(*ins, slice(0, DEPTH), full_l), "gx", _shift(nx, -1))
    hxm = lax.ppermute(_message(*ins, slice(rows - DEPTH, rows), full_l), "gx", _shift(nx, 1))
    hyp = lax.ppermute(_message(*ins, full_r, lo_l), "gy", _shift(ny, -1))
    hym = lax.ppermute(_message(*ins, full_r, hi_l), "gy", _shift(ny, 1))
    c_lo = jnp.concatenate([hxp[:, :, lo_l], hxm[:, :, lo_l]], axis=1)
    c_hi = jnp.concatenate([hxp[:, :, hi_l], hxm[:, :, hi_l]], axis=1)
    cp = lax.ppermute(c_lo, "gy", _shift(ny, -1))
    cm = lax.ppermute(c_hi, "gy", _shift(ny, 1))
    erows = rows + 2 * DEPTH
    eflat = flat + 2 * yw
    ext = (19, erows, eflat)
    args = [saved_pops, seed_adjoint, solid_label, design_mask, design_field, hxp, hxm, hyp, hym, cp, cm]

    def full(shape):
        nd = len(shape)
        return pl.BlockSpec(shape, lambda i, _n=nd: (0,) * _n)

    adjoint, sensitivity = pl.pallas_call(
        _fused_kernel,
        grid=(1,),
        in_specs=[full(a.shape) for a in args],
        out_specs=[full(seed_adjoint.shape), full((rows, flat))],
        out_shape=[
            jax.ShapeDtypeStruct(seed_adjoint.shape, jnp.float32),
            jax.ShapeDtypeStruct((rows, flat), jnp.float32),
        ],
        scratch_shapes=[
            pltpu.VMEM(ext, jnp.float32),
            pltpu.VMEM(ext, jnp.float32),
            pltpu.VMEM(ext, jnp.float32),
            pltpu.VMEM((erows, eflat), jnp.float32),
            pltpu.VMEM((erows, eflat), jnp.float32),
        ],
    )(*args)
    return (adjoint, sensitivity)


def solution(mesh):
    in_specs = (
        P(None, None, "gx", "gy"),
        P(None, "gx", "gy"),
        P("gx", "gy"),
        P("gx", "gy"),
        P("gx", "gy"),
    )
    out_specs = (P(None, "gx", "gy"), P("gx", "gy"))
    return jax.shard_map(body, mesh=mesh, in_specs=in_specs, out_specs=out_specs, check_vma=False)
```

```python
import jax
import jax.numpy as jnp
import numpy as np
from jax import lax
from jax.experimental import pallas as pl
from jax.experimental.pallas import tpu as pltpu
from jax.sharding import PartitionSpec as P

NZ = 32


VELOCITIES = np.array(
    [
        [0, 0, 0],
        [1, 0, 0],
        [-1, 0, 0],
        [0, 1, 0],
        [0, -1, 0],
        [0, 0, 1],
        [0, 0, -1],
        [1, 1, 0],
        [1, -1, 0],
        [-1, 1, 0],
        [-1, -1, 0],
        [1, 0, 1],
        [1, 0, -1],
        [-1, 0, 1],
        [-1, 0, -1],
        [0, 1, 1],
        [0, 1, -1],
        [0, -1, 1],
        [0, -1, -1],
    ]
)
LATTICE_WEIGHTS = np.array([1.0 / 3.0] + [1.0 / 18.0] * 6 + [1.0 / 36.0] * 12)
OPPOSITE = np.array([0, 2, 1, 4, 3, 6, 5, 10, 9, 8, 7, 14, 13, 12, 11, 18, 17, 16, 15])
OMEGA_BASE = 1.0
OMEGA_SPAN = 0.8
SENS_SCALE = 10.0

W32 = [float(np.float32(w)) for w in LATTICE_WEIGHTS]
XP = [i for i in range(19) if VELOCITIES[i, 0] == 1]
XM = [i for i in range(19) if VELOCITIES[i, 0] == -1]
YP = [i for i in range(19) if VELOCITIES[i, 1] == 1]
YM = [i for i in range(19) if VELOCITIES[i, 1] == -1]
LANES = 128


def _velocity(f):
    rho = f[0]
    for i in range(1, 19):
        rho = rho + f[i]
    mom = []
    for a in range(3):
        pos = [f[i] for i in range(19) if VELOCITIES[i, a] > 0]
        neg = [f[i] for i in range(19) if VELOCITIES[i, a] < 0]
        acc = pos[0]
        for x in pos[1:]:
            acc = acc + x
        for x in neg:
            acc = acc - x
        mom.append(acc)
    return rho, [m / rho for m in mom]


def _vjp_core(u, g, rate, solid):
    usq = u[0] * u[0] + u[1] * u[1] + u[2] * u[2]
    base = 1.0 - 1.5 * usq
    fluid = solid == 0
    one_minus = 1.0 - rate
    esum = None
    easum = None
    mb = [None, None, None]
    amp = []
    gf = []
    for i in range(19):
        cvec = [int(c) for c in VELOCITIES[i]]
        p = None
        for a in range(3):
            if cvec[a] == 0:
                continue
            term = u[a] if cvec[a] > 0 else -u[a]
            p = term if p is None else p + term
        if p is None:
            amp_i = base
        else:
            amp_i = base + (3.0 + 4.5 * p) * p
        amp.append(amp_i)
        gi = jnp.where(fluid, g[i], 0.0)
        gf.append(gi)
        e = (rate * W32[i]) * gi
        esum = e if esum is None else esum + e
        ea = e * amp_i
        easum = ea if easum is None else easum + ea
        if p is not None:
            ep = e * (3.0 + 9.0 * p)
            for a in range(3):
                if cvec[a] == 0:
                    continue
                if mb[a] is None:
                    mb[a] = ep if cvec[a] > 0 else -ep
                else:
                    mb[a] = mb[a] + ep if cvec[a] > 0 else mb[a] - ep
    mb = [mb[a] - 3.0 * u[a] * esum for a in range(3)]
    rhobar = easum - (mb[0] * u[0] + mb[1] * u[1] + mb[2] * u[2])
    out = []
    for i in range(19):
        cvec = [int(c) for c in VELOCITIES[i]]
        val = one_minus * gf[i] + rhobar
        for a in range(3):
            if cvec[a] > 0:
                val = val + mb[a]
            elif cvec[a] < 0:
                val = val - mb[a]
        out.append(jnp.where(fluid, val, g[int(OPPOSITE[i])]))
    return out, amp, gf


def _collide_vjp(f, g, rate, solid):
    rho, u = _velocity(f)
    out, amp, gf = _vjp_core(u, g, rate, solid)
    rbar = None
    for i in range(19):
        feq = W32[i] * rho * amp[i]
        t = gf[i] * (feq - f[i])
        rbar = t if rbar is None else rbar + t
    return out, rbar


DEPTH = 4


def _pull_all(a_ref, p_ref):
    _, rows, flat = a_ref.shape
    zl = lax.broadcasted_iota(jnp.int32, (rows, flat), 1) % NZ
    for i in range(19):
        cx, cy, cz = (int(c) for c in VELOCITIES[i])
        v = a_ref[i]
        if cx != 0:
            v = pltpu.roll(v, (rows - cx) % rows, 0)
        if cy != 0:
            v = pltpu.roll(v, (flat - cy * NZ) % flat, 1)
        if cz == 1:
            v = jnp.where(zl == NZ - 1, pltpu.roll(v, NZ - 1, 1), pltpu.roll(v, flat - 1, 1))
        elif cz == -1:
            v = jnp.where(zl == 0, pltpu.roll(v, flat - NZ + 1, 1), pltpu.roll(v, 1, 1))
        p_ref[i] = v


def _fill_ext(dst, own, hxp, hxm, hyp, hym, cp, cm, rows, flat):
    yw = DEPTH * NZ
    if own is not None:
        dst[0:rows, 0:flat] = own
    dst[rows : rows + DEPTH, 0:flat] = hxp
    dst[rows + DEPTH : rows + 2 * DEPTH, 0:flat] = hxm
    dst[0:rows, flat : flat + yw] = hyp
    dst[rows : rows + 2 * DEPTH, flat : flat + yw] = cp
    dst[0:rows, flat + yw : flat + 2 * yw] = hym
    dst[rows : rows + 2 * DEPTH, flat + yw : flat + 2 * yw] = cm


def _fused_kernel(pops_ref, seed_ref, solid_ref, mask_ref, field_ref, hxp, hxm, hyp, hym, cp, cm,
                  adj_out, sens_out, a_ref, p_ref, u_ref, rate_ref, solid_ext):
    steps = pops_ref.shape[0]
    _, rows, flat = seed_ref.shape
    erows, eflat = a_ref.shape[1], a_ref.shape[2]
    nfield = hxp.shape[0]
    mask_all = mask_ref[...].astype(jnp.float32)
    rate_own = OMEGA_BASE + OMEGA_SPAN * field_ref[...] * mask_all
    halo = lambda k, scale=None: [
        h[k] if scale is None else h[k] * scale for h in (hxp, hxm, hyp, hym, cp, cm)
    ]
    _fill_ext(rate_ref, rate_own, *halo(nfield - 2), rows, flat)
    _fill_ext(solid_ext, solid_ref[...].astype(jnp.float32), *halo(nfield - 1), rows, flat)
    for i in range(19):
        _fill_ext(a_ref.at[i], seed_ref[i], *halo(i), rows, flat)
    sens_out[...] = jnp.zeros(sens_out.shape, jnp.float32)
    row_tiles = rows // 8
    lane_tiles = flat // LANES
    ext_lane_tiles = eflat // LANES
    n_own = row_tiles * lane_tiles
    n_halo_rows = (erows - rows) // 8 * lane_tiles
    n_halo = n_halo_rows + (erows // 8) * (ext_lane_tiles - lane_tiles)

    def chunk(step, r0, l0, write_ref, own):
        rs = pl.ds(r0, 8)
        ls = pl.ds(l0, LANES)
        g = [p_ref[i, rs, ls] for i in range(19)]
        solid = solid_ext[rs, ls]
        solid_i = jnp.where(solid > 0.5, 1, 0)
        rate = rate_ref[rs, ls]
        if own:
            f = [pops_ref[step, i, rs, ls].astype(jnp.float32) * W32[i] for i in range(19)]
            new, rbar = _collide_vjp(f, g, rate, solid_i)
            mask = mask_ref[rs, ls].astype(jnp.float32)
            contrib = SENS_SCALE * OMEGA_SPAN * mask * jnp.where(solid_i == 0, rbar, 0.0)
            sens_out[rs, ls] = sens_out[rs, ls] + contrib
        else:
            u = [u_ref[a, rs, ls] for a in range(3)]
            new, _, _ = _vjp_core(u, g, rate, solid_i)
        for i in range(19):
            write_ref[i, rs, ls] = new[i]

    for n, step in enumerate(reversed(range(steps))):
        last = step == 0
        if not last:
            for a in range(3):
                _fill_ext(u_ref.at[a], None, *halo(19 + 3 * n + a), rows, flat)
        _pull_all(a_ref, p_ref)
        write_ref = adj_out if last else a_ref

        def own_body(c, carry, write_ref=write_ref):
            r0 = pl.multiple_of((c // lane_tiles) * 8, 8)
            l0 = pl.multiple_of((c % lane_tiles) * LANES, LANES)
            chunk(step, r0, l0, write_ref, True)
            return carry

        lax.fori_loop(0, n_own, own_body, 0)
        if not last:

            def halo_body(c, carry):
                c2 = c - n_halo_rows
                ext_w = ext_lane_tiles - lane_tiles
                r = jnp.where(c < n_halo_rows, rows // 8 + c // lane_tiles, c2 // ext_w)
                t = jnp.where(c < n_halo_rows, c % lane_tiles, lane_tiles + c2 % ext_w)
                chunk(step, pl.multiple_of(r * 8, 8), pl.multiple_of(t * LANES, LANES), a_ref, False)
                return carry

            lax.fori_loop(0, n_halo, halo_body, 0)


def _message(saved_pops, seed, solid, mask, field, rs, ls):
    steps = saved_pops.shape[0]
    rate = OMEGA_BASE + OMEGA_SPAN * field[rs, ls] * mask[rs, ls].astype(jnp.float32)
    parts = [seed[:, rs, ls]]
    for s in reversed(range(1, steps)):
        f = [saved_pops[s, i][rs, ls].astype(jnp.float32) * W32[i] for i in range(19)]
        parts += [u[None] for u in _velocity(f)[1]]
    parts += [rate[None], solid[rs, ls].astype(jnp.float32)[None]]
    return jnp.concatenate(parts, axis=0)


def _shift(n, d):
    return [(i, (i + d) % n) for i in range(n)]


def body(saved_pops, seed_adjoint, solid_label, design_mask, design_field):
    nx = lax.axis_size("gx")
    ny = lax.axis_size("gy")
    _, rows, flat = seed_adjoint.shape
    yw = DEPTH * NZ
    ins = (saved_pops, seed_adjoint, solid_label, design_mask, design_field)
    full_r, full_l = slice(0, rows), slice(0, flat)
    lo_l, hi_l = slice(0, yw), slice(flat - yw, flat)
    hxp = lax.ppermute(_message(*ins, slice(0, DEPTH), full_l), "gx", _shift(nx, -1))
    hxm = lax.ppermute(_message(*ins, slice(rows - DEPTH, rows), full_l), "gx", _shift(nx, 1))
    hyp = lax.ppermute(_message(*ins, full_r, lo_l), "gy", _shift(ny, -1))
    hym = lax.ppermute(_message(*ins, full_r, hi_l), "gy", _shift(ny, 1))
    c_lo = jnp.concatenate([hxp[:, :, lo_l], hxm[:, :, lo_l]], axis=1)
    c_hi = jnp.concatenate([hxp[:, :, hi_l], hxm[:, :, hi_l]], axis=1)
    cp = lax.ppermute(c_lo, "gy", _shift(ny, -1))
    cm = lax.ppermute(c_hi, "gy", _shift(ny, 1))
    erows = rows + 2 * DEPTH
    eflat = flat + 2 * yw
    ext = (19, erows, eflat)
    args = [saved_pops, seed_adjoint, solid_label, design_mask, design_field, hxp, hxm, hyp, hym, cp, cm]

    def full(shape):
        nd = len(shape)
        return pl.BlockSpec(shape, lambda i, _n=nd: (0,) * _n)

    adjoint, sensitivity = pl.pallas_call(
        _fused_kernel,
        grid=(1,),
        in_specs=[full(a.shape) for a in args],
        out_specs=[full(seed_adjoint.shape), full((rows, flat))],
        out_shape=[
            jax.ShapeDtypeStruct(seed_adjoint.shape, jnp.float32),
            jax.ShapeDtypeStruct((rows, flat), jnp.float32),
        ],
        scratch_shapes=[
            pltpu.VMEM(ext, jnp.float32),
            pltpu.VMEM(ext, jnp.float32),
            pltpu.VMEM((3, erows, eflat), jnp.float32),
            pltpu.VMEM((erows, eflat), jnp.float32),
            pltpu.VMEM((erows, eflat), jnp.float32),
        ],
    )(*args)
    return (adjoint, sensitivity)


def solution(mesh):
    in_specs = (
        P(None, None, "gx", "gy"),
        P(None, "gx", "gy"),
        P("gx", "gy"),
        P("gx", "gy"),
        P("gx", "gy"),
    )
    out_specs = (P(None, "gx", "gy"), P("gx", "gy"))
    return jax.shard_map(body, mesh=mesh, in_specs=in_specs, out_specs=out_specs, check_vma=False)
```

```python
import jax
import jax.numpy as jnp
import numpy as np
from jax import lax
from jax.experimental import pallas as pl
from jax.experimental.pallas import tpu as pltpu
from jax.sharding import PartitionSpec as P

NZ = 32


VELOCITIES = np.array(
    [
        [0, 0, 0],
        [1, 0, 0],
        [-1, 0, 0],
        [0, 1, 0],
        [0, -1, 0],
        [0, 0, 1],
        [0, 0, -1],
        [1, 1, 0],
        [1, -1, 0],
        [-1, 1, 0],
        [-1, -1, 0],
        [1, 0, 1],
        [1, 0, -1],
        [-1, 0, 1],
        [-1, 0, -1],
        [0, 1, 1],
        [0, 1, -1],
        [0, -1, 1],
        [0, -1, -1],
    ]
)
LATTICE_WEIGHTS = np.array([1.0 / 3.0] + [1.0 / 18.0] * 6 + [1.0 / 36.0] * 12)
OPPOSITE = np.array([0, 2, 1, 4, 3, 6, 5, 10, 9, 8, 7, 14, 13, 12, 11, 18, 17, 16, 15])
OMEGA_BASE = 1.0
OMEGA_SPAN = 0.8
SENS_SCALE = 10.0

W32 = [float(np.float32(w)) for w in LATTICE_WEIGHTS]
XP = [i for i in range(19) if VELOCITIES[i, 0] == 1]
XM = [i for i in range(19) if VELOCITIES[i, 0] == -1]
YP = [i for i in range(19) if VELOCITIES[i, 1] == 1]
YM = [i for i in range(19) if VELOCITIES[i, 1] == -1]
LANES = 128


def _velocity(f):
    rho = f[0]
    for i in range(1, 19):
        rho = rho + f[i]
    mom = []
    for a in range(3):
        pos = [f[i] for i in range(19) if VELOCITIES[i, a] > 0]
        neg = [f[i] for i in range(19) if VELOCITIES[i, a] < 0]
        acc = pos[0]
        for x in pos[1:]:
            acc = acc + x
        for x in neg:
            acc = acc - x
        mom.append(acc)
    return rho, [m / rho for m in mom]


def _vjp_core(u, g, rate, solid):
    usq = u[0] * u[0] + u[1] * u[1] + u[2] * u[2]
    base = 1.0 - 1.5 * usq
    fluid = solid == 0
    one_minus = 1.0 - rate
    esum = None
    easum = None
    mb = [None, None, None]
    amp = []
    gf = []
    for i in range(19):
        cvec = [int(c) for c in VELOCITIES[i]]
        p = None
        for a in range(3):
            if cvec[a] == 0:
                continue
            term = u[a] if cvec[a] > 0 else -u[a]
            p = term if p is None else p + term
        if p is None:
            amp_i = base
        else:
            amp_i = base + (3.0 + 4.5 * p) * p
        amp.append(amp_i)
        gi = jnp.where(fluid, g[i], 0.0)
        gf.append(gi)
        e = (rate * W32[i]) * gi
        esum = e if esum is None else esum + e
        ea = e * amp_i
        easum = ea if easum is None else easum + ea
        if p is not None:
            ep = e * (3.0 + 9.0 * p)
            for a in range(3):
                if cvec[a] == 0:
                    continue
                if mb[a] is None:
                    mb[a] = ep if cvec[a] > 0 else -ep
                else:
                    mb[a] = mb[a] + ep if cvec[a] > 0 else mb[a] - ep
    mb = [mb[a] - 3.0 * u[a] * esum for a in range(3)]
    rhobar = easum - (mb[0] * u[0] + mb[1] * u[1] + mb[2] * u[2])
    out = []
    for i in range(19):
        cvec = [int(c) for c in VELOCITIES[i]]
        val = one_minus * gf[i] + rhobar
        for a in range(3):
            if cvec[a] > 0:
                val = val + mb[a]
            elif cvec[a] < 0:
                val = val - mb[a]
        out.append(jnp.where(fluid, val, g[int(OPPOSITE[i])]))
    return out, amp, gf


def _collide_vjp(f, g, rate, solid):
    rho, u = _velocity(f)
    out, amp, gf = _vjp_core(u, g, rate, solid)
    rbar = None
    for i in range(19):
        feq = W32[i] * rho * amp[i]
        t = gf[i] * (feq - f[i])
        rbar = t if rbar is None else rbar + t
    return out, rbar


DEPTH = 4


def _pull_all(a_ref, p_ref):
    _, rows, flat = a_ref.shape
    zl = lax.broadcasted_iota(jnp.int32, (rows, flat), 1) % NZ
    for i in range(19):
        cx, cy, cz = (int(c) for c in VELOCITIES[i])
        v = a_ref[i]
        if cx != 0:
            v = pltpu.roll(v, (rows - cx) % rows, 0)
        if cy != 0:
            v = pltpu.roll(v, (flat - cy * NZ) % flat, 1)
        if cz == 1:
            v = jnp.where(zl == NZ - 1, pltpu.roll(v, NZ - 1, 1), pltpu.roll(v, flat - 1, 1))
        elif cz == -1:
            v = jnp.where(zl == 0, pltpu.roll(v, flat - NZ + 1, 1), pltpu.roll(v, 1, 1))
        p_ref[i] = v


def _fill_ext(dst, own, hxp, hxm, hyp, hym, cp, cm, rows, flat):
    yw = DEPTH * NZ
    if own is not None:
        dst[0:rows, 0:flat] = own
    dst[rows : rows + DEPTH, 0:flat] = hxp
    dst[rows + DEPTH : rows + 2 * DEPTH, 0:flat] = hxm
    dst[0:rows, flat : flat + yw] = hyp
    dst[rows : rows + 2 * DEPTH, flat : flat + yw] = cp
    dst[0:rows, flat + yw : flat + 2 * yw] = hym
    dst[rows : rows + 2 * DEPTH, flat + yw : flat + 2 * yw] = cm


def _fused_kernel(pops_ref, seed_ref, solid_ref, mask_ref, field_ref, hxp, hxm, hyp, hym, cp, cm,
                  adj_out, sens_out, a_ref, p_ref, u_ref, rate_ref, solid_ext):
    steps = pops_ref.shape[0]
    _, rows, flat = seed_ref.shape
    erows, eflat = a_ref.shape[1], a_ref.shape[2]
    nfield = hxp.shape[0]
    mask_all = mask_ref[...].astype(jnp.float32)
    rate_own = OMEGA_BASE + OMEGA_SPAN * field_ref[...] * mask_all
    halo = lambda k, scale=None: [
        h[k] if scale is None else h[k] * scale for h in (hxp, hxm, hyp, hym, cp, cm)
    ]
    _fill_ext(rate_ref, rate_own, *halo(nfield - 2), rows, flat)
    _fill_ext(solid_ext, solid_ref[...].astype(jnp.float32), *halo(nfield - 1), rows, flat)
    for i in range(19):
        _fill_ext(a_ref.at[i], seed_ref[i], *halo(i), rows, flat)
    sens_out[...] = jnp.zeros(sens_out.shape, jnp.float32)
    row_tiles = rows // 8
    lane_tiles = flat // LANES
    ext_lane_tiles = eflat // LANES
    n_own = row_tiles * lane_tiles
    n_halo_rows = (erows - rows) // 8 * lane_tiles
    n_halo = n_halo_rows + (erows // 8) * (ext_lane_tiles - lane_tiles)

    def chunk(step, r0, l0, write_ref, own):
        rs = pl.ds(r0, 8)
        ls = pl.ds(l0, LANES)
        g = [p_ref[i, rs, ls] for i in range(19)]
        solid = solid_ext[rs, ls]
        solid_i = jnp.where(solid > 0.5, 1, 0)
        rate = rate_ref[rs, ls]
        if own:
            f = [pops_ref[step, i, rs, ls].astype(jnp.float32) * W32[i] for i in range(19)]
            new, rbar = _collide_vjp(f, g, rate, solid_i)
            mask = mask_ref[rs, ls].astype(jnp.float32)
            contrib = SENS_SCALE * OMEGA_SPAN * mask * jnp.where(solid_i == 0, rbar, 0.0)
            sens_out[rs, ls] = sens_out[rs, ls] + contrib
        else:
            u = [u_ref[a, rs, ls] for a in range(3)]
            new, _, _ = _vjp_core(u, g, rate, solid_i)
        for i in range(19):
            write_ref[i, rs, ls] = new[i]

    for n, step in enumerate(reversed(range(steps))):
        last = step == 0
        if not last:
            for a in range(3):
                _fill_ext(u_ref.at[a], None, *halo(19 + 3 * n + a), rows, flat)
        _pull_all(a_ref, p_ref)
        write_ref = adj_out if last else a_ref

        def own_body(c, carry, write_ref=write_ref):
            r0 = pl.multiple_of((c // lane_tiles) * 8, 8)
            l0 = pl.multiple_of((c % lane_tiles) * LANES, LANES)
            chunk(step, r0, l0, write_ref, True)
            return carry

        lax.fori_loop(0, n_own, own_body, 0)
        if not last:

            def halo_body(c, carry):
                c2 = c - n_halo_rows
                ext_w = ext_lane_tiles - lane_tiles
                r = jnp.where(c < n_halo_rows, rows // 8 + c // lane_tiles, c2 // ext_w)
                t = jnp.where(c < n_halo_rows, c % lane_tiles, lane_tiles + c2 % ext_w)
                chunk(step, pl.multiple_of(r * 8, 8), pl.multiple_of(t * LANES, LANES), a_ref, False)
                return carry

            lax.fori_loop(0, n_halo, halo_body, 0)


def _prep_kernel(pops_ref, seed_ref, solid_ref, mask_ref, field_ref, x_lo, x_hi, y_lo, y_hi, u_ref):
    steps = pops_ref.shape[0]
    _, rows, flat = seed_ref.shape
    yw = DEPTH * NZ
    for n, step in enumerate(reversed(range(1, steps))):
        for t in range(flat // LANES):
            sl = slice(LANES * t, LANES * (t + 1))
            f = [pops_ref[step, i, :, sl].astype(jnp.float32) * W32[i] for i in range(19)]
            _, u = _velocity(f)
            for a in range(3):
                u_ref[3 * n + a, :, sl] = u[a]
    nu = 3 * (steps - 1)
    rate = OMEGA_BASE + OMEGA_SPAN * field_ref[...] * mask_ref[...].astype(jnp.float32)
    solid = solid_ref[...].astype(jnp.float32)
    fields = [lambda rs, ls, i=i: seed_ref[i, rs, ls] for i in range(19)]
    fields += [lambda rs, ls, k=k: u_ref[k, rs, ls] for k in range(nu)]
    fields += [lambda rs, ls: rate[rs, ls], lambda rs, ls: solid[rs, ls]]
    for k, get in enumerate(fields):
        x_lo[k] = get(slice(0, DEPTH), slice(0, flat))
        x_hi[k] = get(slice(rows - DEPTH, rows), slice(0, flat))
        y_lo[k] = get(slice(0, rows), slice(0, yw))
        y_hi[k] = get(slice(0, rows), slice(flat - yw, flat))


def _messages(saved_pops, seed, solid, mask, field):
    steps = saved_pops.shape[0]
    _, rows, flat = seed.shape
    nfield = 19 + 3 * (steps - 1) + 2
    yw = DEPTH * NZ
    shapes = [(nfield, DEPTH, flat), (nfield, DEPTH, flat), (nfield, rows, yw), (nfield, rows, yw)]
    args = [saved_pops, seed, solid, mask, field]

    def full(shape):
        nd = len(shape)
        return pl.BlockSpec(shape, lambda i, _n=nd: (0,) * _n)

    return pl.pallas_call(
        _prep_kernel,
        grid=(1,),
        in_specs=[full(a.shape) for a in args],
        out_specs=[full(sh) for sh in shapes],
        out_shape=[jax.ShapeDtypeStruct(sh, jnp.float32) for sh in shapes],
        scratch_shapes=[pltpu.VMEM((3 * (steps - 1), rows, flat), jnp.float32)],
    )(*args)


def _shift(n, d):
    return [(i, (i + d) % n) for i in range(n)]


def body(saved_pops, seed_adjoint, solid_label, design_mask, design_field):
    nx = lax.axis_size("gx")
    ny = lax.axis_size("gy")
    _, rows, flat = seed_adjoint.shape
    yw = DEPTH * NZ
    lo_l, hi_l = slice(0, yw), slice(flat - yw, flat)
    x_lo, x_hi, y_lo, y_hi = _messages(saved_pops, seed_adjoint, solid_label, design_mask, design_field)
    hxp = lax.ppermute(x_lo, "gx", _shift(nx, -1))
    hxm = lax.ppermute(x_hi, "gx", _shift(nx, 1))
    hyp = lax.ppermute(y_lo, "gy", _shift(ny, -1))
    hym = lax.ppermute(y_hi, "gy", _shift(ny, 1))
    c_lo = jnp.concatenate([hxp[:, :, lo_l], hxm[:, :, lo_l]], axis=1)
    c_hi = jnp.concatenate([hxp[:, :, hi_l], hxm[:, :, hi_l]], axis=1)
    cp = lax.ppermute(c_lo, "gy", _shift(ny, -1))
    cm = lax.ppermute(c_hi, "gy", _shift(ny, 1))
    erows = rows + 2 * DEPTH
    eflat = flat + 2 * yw
    ext = (19, erows, eflat)
    args = [saved_pops, seed_adjoint, solid_label, design_mask, design_field, hxp, hxm, hyp, hym, cp, cm]

    def full(shape):
        nd = len(shape)
        return pl.BlockSpec(shape, lambda i, _n=nd: (0,) * _n)

    adjoint, sensitivity = pl.pallas_call(
        _fused_kernel,
        grid=(1,),
        in_specs=[full(a.shape) for a in args],
        out_specs=[full(seed_adjoint.shape), full((rows, flat))],
        out_shape=[
            jax.ShapeDtypeStruct(seed_adjoint.shape, jnp.float32),
            jax.ShapeDtypeStruct((rows, flat), jnp.float32),
        ],
        scratch_shapes=[
            pltpu.VMEM(ext, jnp.float32),
            pltpu.VMEM(ext, jnp.float32),
            pltpu.VMEM((3, erows, eflat), jnp.float32),
            pltpu.VMEM((erows, eflat), jnp.float32),
            pltpu.VMEM((erows, eflat), jnp.float32),
        ],
    )(*args)
    return (adjoint, sensitivity)


def solution(mesh):
    in_specs = (
        P(None, None, "gx", "gy"),
        P(None, "gx", "gy"),
        P("gx", "gy"),
        P("gx", "gy"),
        P("gx", "gy"),
    )
    out_specs = (P(None, "gx", "gy"), P("gx", "gy"))
    return jax.shard_map(body, mesh=mesh, in_specs=in_specs, out_specs=out_specs, check_vma=False)
```

```python
import jax
import jax.numpy as jnp
import numpy as np
from jax import lax
from jax.experimental import pallas as pl
from jax.experimental.pallas import tpu as pltpu
from jax.sharding import PartitionSpec as P

NZ = 32


VELOCITIES = np.array(
    [
        [0, 0, 0],
        [1, 0, 0],
        [-1, 0, 0],
        [0, 1, 0],
        [0, -1, 0],
        [0, 0, 1],
        [0, 0, -1],
        [1, 1, 0],
        [1, -1, 0],
        [-1, 1, 0],
        [-1, -1, 0],
        [1, 0, 1],
        [1, 0, -1],
        [-1, 0, 1],
        [-1, 0, -1],
        [0, 1, 1],
        [0, 1, -1],
        [0, -1, 1],
        [0, -1, -1],
    ]
)
LATTICE_WEIGHTS = np.array([1.0 / 3.0] + [1.0 / 18.0] * 6 + [1.0 / 36.0] * 12)
OPPOSITE = np.array([0, 2, 1, 4, 3, 6, 5, 10, 9, 8, 7, 14, 13, 12, 11, 18, 17, 16, 15])
OMEGA_BASE = 1.0
OMEGA_SPAN = 0.8
SENS_SCALE = 10.0

W32 = [float(np.float32(w)) for w in LATTICE_WEIGHTS]
XP = [i for i in range(19) if VELOCITIES[i, 0] == 1]
XM = [i for i in range(19) if VELOCITIES[i, 0] == -1]
YP = [i for i in range(19) if VELOCITIES[i, 1] == 1]
YM = [i for i in range(19) if VELOCITIES[i, 1] == -1]
LANES = 128


def _velocity(f):
    rho = f[0]
    for i in range(1, 19):
        rho = rho + f[i]
    mom = []
    for a in range(3):
        pos = [f[i] for i in range(19) if VELOCITIES[i, a] > 0]
        neg = [f[i] for i in range(19) if VELOCITIES[i, a] < 0]
        acc = pos[0]
        for x in pos[1:]:
            acc = acc + x
        for x in neg:
            acc = acc - x
        mom.append(acc)
    return rho, [m / rho for m in mom]


def _vjp_core(u, g, rate, solid):
    usq = u[0] * u[0] + u[1] * u[1] + u[2] * u[2]
    base = 1.0 - 1.5 * usq
    fluid = solid == 0
    one_minus = 1.0 - rate
    esum = None
    easum = None
    mb = [None, None, None]
    amp = []
    gf = []
    for i in range(19):
        cvec = [int(c) for c in VELOCITIES[i]]
        p = None
        for a in range(3):
            if cvec[a] == 0:
                continue
            term = u[a] if cvec[a] > 0 else -u[a]
            p = term if p is None else p + term
        if p is None:
            amp_i = base
        else:
            amp_i = base + (3.0 + 4.5 * p) * p
        amp.append(amp_i)
        gi = jnp.where(fluid, g[i], 0.0)
        gf.append(gi)
        e = (rate * W32[i]) * gi
        esum = e if esum is None else esum + e
        ea = e * amp_i
        easum = ea if easum is None else easum + ea
        if p is not None:
            ep = e * (3.0 + 9.0 * p)
            for a in range(3):
                if cvec[a] == 0:
                    continue
                if mb[a] is None:
                    mb[a] = ep if cvec[a] > 0 else -ep
                else:
                    mb[a] = mb[a] + ep if cvec[a] > 0 else mb[a] - ep
    mb = [mb[a] - 3.0 * u[a] * esum for a in range(3)]
    rhobar = easum - (mb[0] * u[0] + mb[1] * u[1] + mb[2] * u[2])
    out = []
    for i in range(19):
        cvec = [int(c) for c in VELOCITIES[i]]
        val = one_minus * gf[i] + rhobar
        for a in range(3):
            if cvec[a] > 0:
                val = val + mb[a]
            elif cvec[a] < 0:
                val = val - mb[a]
        out.append(jnp.where(fluid, val, g[int(OPPOSITE[i])]))
    return out, amp, gf


def _collide_vjp(f, g, rate, solid):
    rho, u = _velocity(f)
    out, amp, gf = _vjp_core(u, g, rate, solid)
    rbar = None
    for i in range(19):
        feq = W32[i] * rho * amp[i]
        t = gf[i] * (feq - f[i])
        rbar = t if rbar is None else rbar + t
    return out, rbar


DEPTH = 4


def _pull_all(a_ref, p_ref):
    _, rows, flat = a_ref.shape
    zl = lax.broadcasted_iota(jnp.int32, (rows, flat), 1) % NZ
    for i in range(19):
        cx, cy, cz = (int(c) for c in VELOCITIES[i])
        v = a_ref[i]
        if cx != 0:
            v = pltpu.roll(v, (rows - cx) % rows, 0)
        if cy != 0:
            v = pltpu.roll(v, (flat - cy * NZ) % flat, 1)
        if cz == 1:
            v = jnp.where(zl == NZ - 1, pltpu.roll(v, NZ - 1, 1), pltpu.roll(v, flat - 1, 1))
        elif cz == -1:
            v = jnp.where(zl == 0, pltpu.roll(v, flat - NZ + 1, 1), pltpu.roll(v, 1, 1))
        p_ref[i] = v


def _fill_ext(dst, own, hxp, hxm, hyp, hym, rows, flat):
    yw = DEPTH * NZ
    if own is not None:
        dst[0:rows, 0:flat] = own
    dst[rows : rows + DEPTH, 0:flat] = hxp
    dst[rows + DEPTH : rows + 2 * DEPTH, 0:flat] = hxm
    dst[:, flat : flat + yw] = hyp
    dst[:, flat + yw : flat + 2 * yw] = hym


def _fused_kernel(pops_ref, seed_ref, solid_ref, mask_ref, field_ref, hxp, hxm, hyp, hym,
                  adj_out, sens_out, a_ref, p_ref, u_ref, rate_ref, solid_ext):
    steps = pops_ref.shape[0]
    _, rows, flat = seed_ref.shape
    erows, eflat = a_ref.shape[1], a_ref.shape[2]
    nfield = hxp.shape[0]
    mask_all = mask_ref[...].astype(jnp.float32)
    rate_own = OMEGA_BASE + OMEGA_SPAN * field_ref[...] * mask_all
    halo = lambda k, scale=None: [
        h[k] if scale is None else h[k] * scale for h in (hxp, hxm, hyp, hym)
    ]
    _fill_ext(rate_ref, rate_own, *halo(nfield - 2), rows, flat)
    _fill_ext(solid_ext, solid_ref[...].astype(jnp.float32), *halo(nfield - 1), rows, flat)
    for i in range(19):
        _fill_ext(a_ref.at[i], seed_ref[i], *halo(i), rows, flat)
    sens_out[...] = jnp.zeros(sens_out.shape, jnp.float32)
    row_tiles = rows // 8
    lane_tiles = flat // LANES
    ext_lane_tiles = eflat // LANES
    n_own = row_tiles * lane_tiles
    n_halo_rows = (erows - rows) // 8 * lane_tiles
    n_halo = n_halo_rows + (erows // 8) * (ext_lane_tiles - lane_tiles)

    def chunk(step, r0, l0, write_ref, own):
        rs = pl.ds(r0, 8)
        ls = pl.ds(l0, LANES)
        g = [p_ref[i, rs, ls] for i in range(19)]
        solid = solid_ext[rs, ls]
        solid_i = jnp.where(solid > 0.5, 1, 0)
        rate = rate_ref[rs, ls]
        if own:
            f = [pops_ref[step, i, rs, ls].astype(jnp.float32) * W32[i] for i in range(19)]
            new, rbar = _collide_vjp(f, g, rate, solid_i)
            mask = mask_ref[rs, ls].astype(jnp.float32)
            contrib = SENS_SCALE * OMEGA_SPAN * mask * jnp.where(solid_i == 0, rbar, 0.0)
            sens_out[rs, ls] = sens_out[rs, ls] + contrib
        else:
            u = [u_ref[a, rs, ls] for a in range(3)]
            new, _, _ = _vjp_core(u, g, rate, solid_i)
        for i in range(19):
            write_ref[i, rs, ls] = new[i]

    for n, step in enumerate(reversed(range(steps))):
        last = step == 0
        if not last:
            for a in range(3):
                _fill_ext(u_ref.at[a], None, *halo(19 + 3 * n + a), rows, flat)
        _pull_all(a_ref, p_ref)
        write_ref = adj_out if last else a_ref

        def own_body(c, carry, write_ref=write_ref):
            r0 = pl.multiple_of((c // lane_tiles) * 8, 8)
            l0 = pl.multiple_of((c % lane_tiles) * LANES, LANES)
            chunk(step, r0, l0, write_ref, True)
            return carry

        lax.fori_loop(0, n_own, own_body, 0)
        if not last:

            def halo_body(c, carry):
                c2 = c - n_halo_rows
                ext_w = ext_lane_tiles - lane_tiles
                r = jnp.where(c < n_halo_rows, rows // 8 + c // lane_tiles, c2 // ext_w)
                t = jnp.where(c < n_halo_rows, c % lane_tiles, lane_tiles + c2 % ext_w)
                chunk(step, pl.multiple_of(r * 8, 8), pl.multiple_of(t * LANES, LANES), a_ref, False)
                return carry

            lax.fori_loop(0, n_halo, halo_body, 0)


def _prep_kernel(pops_ref, seed_ref, solid_ref, mask_ref, field_ref, x_lo, x_hi, y_lo, y_hi, u_ref):
    steps = pops_ref.shape[0]
    _, rows, flat = seed_ref.shape
    yw = DEPTH * NZ
    for n, step in enumerate(reversed(range(1, steps))):
        for t in range(flat // LANES):
            sl = slice(LANES * t, LANES * (t + 1))
            f = [pops_ref[step, i, :, sl].astype(jnp.float32) * W32[i] for i in range(19)]
            _, u = _velocity(f)
            for a in range(3):
                u_ref[3 * n + a, :, sl] = u[a]
    nu = 3 * (steps - 1)
    rate = OMEGA_BASE + OMEGA_SPAN * field_ref[...] * mask_ref[...].astype(jnp.float32)
    solid = solid_ref[...].astype(jnp.float32)
    fields = [lambda rs, ls, i=i: seed_ref[i, rs, ls] for i in range(19)]
    fields += [lambda rs, ls, k=k: u_ref[k, rs, ls] for k in range(nu)]
    fields += [lambda rs, ls: rate[rs, ls], lambda rs, ls: solid[rs, ls]]
    for k, get in enumerate(fields):
        x_lo[k] = get(slice(0, DEPTH), slice(0, flat))
        x_hi[k] = get(slice(rows - DEPTH, rows), slice(0, flat))
        y_lo[k] = get(slice(0, rows), slice(0, yw))
        y_hi[k] = get(slice(0, rows), slice(flat - yw, flat))


def _messages(saved_pops, seed, solid, mask, field):
    steps = saved_pops.shape[0]
    _, rows, flat = seed.shape
    nfield = 19 + 3 * (steps - 1) + 2
    yw = DEPTH * NZ
    shapes = [(nfield, DEPTH, flat), (nfield, DEPTH, flat), (nfield, rows, yw), (nfield, rows, yw)]
    args = [saved_pops, seed, solid, mask, field]

    def full(shape):
        nd = len(shape)
        return pl.BlockSpec(shape, lambda i, _n=nd: (0,) * _n)

    return pl.pallas_call(
        _prep_kernel,
        grid=(1,),
        in_specs=[full(a.shape) for a in args],
        out_specs=[full(sh) for sh in shapes],
        out_shape=[jax.ShapeDtypeStruct(sh, jnp.float32) for sh in shapes],
        scratch_shapes=[pltpu.VMEM((3 * (steps - 1), rows, flat), jnp.float32)],
    )(*args)


def _shift(n, d):
    return [(i, (i + d) % n) for i in range(n)]


def body(saved_pops, seed_adjoint, solid_label, design_mask, design_field):
    nx = lax.axis_size("gx")
    ny = lax.axis_size("gy")
    _, rows, flat = seed_adjoint.shape
    yw = DEPTH * NZ
    lo_l, hi_l = slice(0, yw), slice(flat - yw, flat)
    x_lo, x_hi, y_lo, y_hi = _messages(saved_pops, seed_adjoint, solid_label, design_mask, design_field)
    hxp = lax.ppermute(x_lo, "gx", _shift(nx, -1))
    hxm = lax.ppermute(x_hi, "gx", _shift(nx, 1))
    col_lo = jnp.concatenate([y_lo, hxp[:, :, lo_l], hxm[:, :, lo_l]], axis=1)
    col_hi = jnp.concatenate([y_hi, hxp[:, :, hi_l], hxm[:, :, hi_l]], axis=1)
    hyp = lax.ppermute(col_lo, "gy", _shift(ny, -1))
    hym = lax.ppermute(col_hi, "gy", _shift(ny, 1))
    erows = rows + 2 * DEPTH
    eflat = flat + 2 * yw
    ext = (19, erows, eflat)
    args = [saved_pops, seed_adjoint, solid_label, design_mask, design_field, hxp, hxm, hyp, hym]

    def full(shape):
        nd = len(shape)
        return pl.BlockSpec(shape, lambda i, _n=nd: (0,) * _n)

    adjoint, sensitivity = pl.pallas_call(
        _fused_kernel,
        grid=(1,),
        in_specs=[full(a.shape) for a in args],
        out_specs=[full(seed_adjoint.shape), full((rows, flat))],
        out_shape=[
            jax.ShapeDtypeStruct(seed_adjoint.shape, jnp.float32),
            jax.ShapeDtypeStruct((rows, flat), jnp.float32),
        ],
        scratch_shapes=[
            pltpu.VMEM(ext, jnp.float32),
            pltpu.VMEM(ext, jnp.float32),
            pltpu.VMEM((3, erows, eflat), jnp.float32),
            pltpu.VMEM((erows, eflat), jnp.float32),
            pltpu.VMEM((erows, eflat), jnp.float32),
        ],
    )(*args)
    return (adjoint, sensitivity)


def solution(mesh):
    in_specs = (
        P(None, None, "gx", "gy"),
        P(None, "gx", "gy"),
        P("gx", "gy"),
        P("gx", "gy"),
        P("gx", "gy"),
    )
    out_specs = (P(None, "gx", "gy"), P("gx", "gy"))
    return jax.shard_map(body, mesh=mesh, in_specs=in_specs, out_specs=out_specs, check_vma=False)
```

```python
import jax
import jax.numpy as jnp
import numpy as np
from jax import lax
from jax.experimental import pallas as pl
from jax.experimental.pallas import tpu as pltpu
from jax.sharding import PartitionSpec as P

NZ = 32


VELOCITIES = np.array(
    [
        [0, 0, 0],
        [1, 0, 0],
        [-1, 0, 0],
        [0, 1, 0],
        [0, -1, 0],
        [0, 0, 1],
        [0, 0, -1],
        [1, 1, 0],
        [1, -1, 0],
        [-1, 1, 0],
        [-1, -1, 0],
        [1, 0, 1],
        [1, 0, -1],
        [-1, 0, 1],
        [-1, 0, -1],
        [0, 1, 1],
        [0, 1, -1],
        [0, -1, 1],
        [0, -1, -1],
    ]
)
LATTICE_WEIGHTS = np.array([1.0 / 3.0] + [1.0 / 18.0] * 6 + [1.0 / 36.0] * 12)
OPPOSITE = np.array([0, 2, 1, 4, 3, 6, 5, 10, 9, 8, 7, 14, 13, 12, 11, 18, 17, 16, 15])
OMEGA_BASE = 1.0
OMEGA_SPAN = 0.8
SENS_SCALE = 10.0

W32 = [float(np.float32(w)) for w in LATTICE_WEIGHTS]
XP = [i for i in range(19) if VELOCITIES[i, 0] == 1]
XM = [i for i in range(19) if VELOCITIES[i, 0] == -1]
YP = [i for i in range(19) if VELOCITIES[i, 1] == 1]
YM = [i for i in range(19) if VELOCITIES[i, 1] == -1]
LANES = 128


def _velocity(f):
    rho = f[0]
    for i in range(1, 19):
        rho = rho + f[i]
    mom = []
    for a in range(3):
        pos = [f[i] for i in range(19) if VELOCITIES[i, a] > 0]
        neg = [f[i] for i in range(19) if VELOCITIES[i, a] < 0]
        acc = pos[0]
        for x in pos[1:]:
            acc = acc + x
        for x in neg:
            acc = acc - x
        mom.append(acc)
    return rho, [m / rho for m in mom]


def _vjp_core(u, g, rate, solid):
    usq = u[0] * u[0] + u[1] * u[1] + u[2] * u[2]
    base = 1.0 - 1.5 * usq
    fluid = solid == 0
    one_minus = 1.0 - rate
    esum = None
    easum = None
    mb = [None, None, None]
    amp = []
    gf = []
    for i in range(19):
        cvec = [int(c) for c in VELOCITIES[i]]
        p = None
        for a in range(3):
            if cvec[a] == 0:
                continue
            term = u[a] if cvec[a] > 0 else -u[a]
            p = term if p is None else p + term
        if p is None:
            amp_i = base
        else:
            amp_i = base + (3.0 + 4.5 * p) * p
        amp.append(amp_i)
        gi = jnp.where(fluid, g[i], 0.0)
        gf.append(gi)
        e = (rate * W32[i]) * gi
        esum = e if esum is None else esum + e
        ea = e * amp_i
        easum = ea if easum is None else easum + ea
        if p is not None:
            ep = e * (3.0 + 9.0 * p)
            for a in range(3):
                if cvec[a] == 0:
                    continue
                if mb[a] is None:
                    mb[a] = ep if cvec[a] > 0 else -ep
                else:
                    mb[a] = mb[a] + ep if cvec[a] > 0 else mb[a] - ep
    mb = [mb[a] - 3.0 * u[a] * esum for a in range(3)]
    rhobar = easum - (mb[0] * u[0] + mb[1] * u[1] + mb[2] * u[2])
    out = []
    for i in range(19):
        cvec = [int(c) for c in VELOCITIES[i]]
        val = one_minus * gf[i] + rhobar
        for a in range(3):
            if cvec[a] > 0:
                val = val + mb[a]
            elif cvec[a] < 0:
                val = val - mb[a]
        out.append(jnp.where(fluid, val, g[int(OPPOSITE[i])]))
    return out, amp, gf


def _collide_vjp(f, g, rate, solid):
    rho, u = _velocity(f)
    out, amp, gf = _vjp_core(u, g, rate, solid)
    rbar = None
    for i in range(19):
        feq = W32[i] * rho * amp[i]
        t = gf[i] * (feq - f[i])
        rbar = t if rbar is None else rbar + t
    return out, rbar


DEPTH = 4


def _pull_all(a_ref, p_ref):
    _, rows, flat = a_ref.shape
    zl = lax.broadcasted_iota(jnp.int32, (rows, flat), 1) % NZ
    for i in range(19):
        cx, cy, cz = (int(c) for c in VELOCITIES[i])
        v = a_ref[i]
        if cx != 0:
            v = pltpu.roll(v, (rows - cx) % rows, 0)
        if cy != 0:
            v = pltpu.roll(v, (flat - cy * NZ) % flat, 1)
        if cz == 1:
            v = jnp.where(zl == NZ - 1, pltpu.roll(v, NZ - 1, 1), pltpu.roll(v, flat - 1, 1))
        elif cz == -1:
            v = jnp.where(zl == 0, pltpu.roll(v, flat - NZ + 1, 1), pltpu.roll(v, 1, 1))
        p_ref[i] = v


def _fill_ext(dst, own, hxp, hxm, hyp, hym, cp, cm, rows, flat):
    yw = DEPTH * NZ
    if own is not None:
        dst[0:rows, 0:flat] = own
    dst[rows : rows + DEPTH, 0:flat] = hxp
    dst[rows + DEPTH : rows + 2 * DEPTH, 0:flat] = hxm
    dst[0:rows, flat : flat + yw] = hyp
    dst[rows : rows + 2 * DEPTH, flat : flat + yw] = cp
    dst[0:rows, flat + yw : flat + 2 * yw] = hym
    dst[rows : rows + 2 * DEPTH, flat + yw : flat + 2 * yw] = cm


def _fused_kernel(pops_ref, seed_ref, solid_ref, mask_ref, field_ref, hxp, hxm, hyp, hym, cp, cm,
                  adj_out, sens_out, a_ref, p_ref, u_ref, rate_ref, solid_ext):
    steps = pops_ref.shape[0]
    _, rows, flat = seed_ref.shape
    erows, eflat = a_ref.shape[1], a_ref.shape[2]
    nfield = hyp.shape[0]
    mask_all = mask_ref[...].astype(jnp.float32)
    rate_own = OMEGA_BASE + OMEGA_SPAN * field_ref[...] * mask_all
    def halo(k, scale=None):
        parts = [
            hxp[DEPTH * k : DEPTH * (k + 1), :],
            hxm[DEPTH * k : DEPTH * (k + 1), :],
            hyp[k],
            hym[k],
            cp[2 * DEPTH * k : 2 * DEPTH * (k + 1), :],
            cm[2 * DEPTH * k : 2 * DEPTH * (k + 1), :],
        ]
        return parts if scale is None else [p * scale for p in parts]
    _fill_ext(rate_ref, rate_own, *halo(nfield - 2), rows, flat)
    _fill_ext(solid_ext, solid_ref[...].astype(jnp.float32), *halo(nfield - 1), rows, flat)
    for i in range(19):
        _fill_ext(a_ref.at[i], seed_ref[i], *halo(i), rows, flat)
    sens_out[...] = jnp.zeros(sens_out.shape, jnp.float32)
    row_tiles = rows // 8
    lane_tiles = flat // LANES
    ext_lane_tiles = eflat // LANES
    n_own = row_tiles * lane_tiles
    n_halo_rows = (erows - rows) // 8 * lane_tiles
    n_halo = n_halo_rows + (erows // 8) * (ext_lane_tiles - lane_tiles)

    def chunk(step, r0, l0, write_ref, own):
        rs = pl.ds(r0, 8)
        ls = pl.ds(l0, LANES)
        g = [p_ref[i, rs, ls] for i in range(19)]
        solid = solid_ext[rs, ls]
        solid_i = jnp.where(solid > 0.5, 1, 0)
        rate = rate_ref[rs, ls]
        if own:
            f = [pops_ref[step, i, rs, ls].astype(jnp.float32) * W32[i] for i in range(19)]
            new, rbar = _collide_vjp(f, g, rate, solid_i)
            mask = mask_ref[rs, ls].astype(jnp.float32)
            contrib = SENS_SCALE * OMEGA_SPAN * mask * jnp.where(solid_i == 0, rbar, 0.0)
            sens_out[rs, ls] = sens_out[rs, ls] + contrib
        else:
            u = [u_ref[a, rs, ls] for a in range(3)]
            new, _, _ = _vjp_core(u, g, rate, solid_i)
        for i in range(19):
            write_ref[i, rs, ls] = new[i]

    for n, step in enumerate(reversed(range(steps))):
        last = step == 0
        if not last:
            for a in range(3):
                _fill_ext(u_ref.at[a], None, *halo(19 + 3 * n + a), rows, flat)
        _pull_all(a_ref, p_ref)
        write_ref = adj_out if last else a_ref

        def own_body(c, carry, write_ref=write_ref):
            r0 = pl.multiple_of((c // lane_tiles) * 8, 8)
            l0 = pl.multiple_of((c % lane_tiles) * LANES, LANES)
            chunk(step, r0, l0, write_ref, True)
            return carry

        lax.fori_loop(0, n_own, own_body, 0)
        if not last:

            def halo_body(c, carry):
                c2 = c - n_halo_rows
                ext_w = ext_lane_tiles - lane_tiles
                r = jnp.where(c < n_halo_rows, rows // 8 + c // lane_tiles, c2 // ext_w)
                t = jnp.where(c < n_halo_rows, c % lane_tiles, lane_tiles + c2 % ext_w)
                chunk(step, pl.multiple_of(r * 8, 8), pl.multiple_of(t * LANES, LANES), a_ref, False)
                return carry

            lax.fori_loop(0, n_halo, halo_body, 0)


def _prep_kernel(pops_ref, seed_ref, solid_ref, mask_ref, field_ref, x_lo, x_hi, y_lo, y_hi, u_ref):
    steps = pops_ref.shape[0]
    _, rows, flat = seed_ref.shape
    yw = DEPTH * NZ
    for n, step in enumerate(reversed(range(1, steps))):
        for t in range(flat // LANES):
            sl = slice(LANES * t, LANES * (t + 1))
            f = [pops_ref[step, i, :, sl].astype(jnp.float32) * W32[i] for i in range(19)]
            _, u = _velocity(f)
            for a in range(3):
                u_ref[3 * n + a, :, sl] = u[a]
    nu = 3 * (steps - 1)
    rate = OMEGA_BASE + OMEGA_SPAN * field_ref[...] * mask_ref[...].astype(jnp.float32)
    solid = solid_ref[...].astype(jnp.float32)
    fields = [lambda rs, ls, i=i: seed_ref[i, rs, ls] for i in range(19)]
    fields += [lambda rs, ls, k=k: u_ref[k, rs, ls] for k in range(nu)]
    fields += [lambda rs, ls: rate[rs, ls], lambda rs, ls: solid[rs, ls]]
    for k, get in enumerate(fields):
        x_lo[DEPTH * k : DEPTH * (k + 1), :] = get(slice(0, DEPTH), slice(0, flat))
        x_hi[DEPTH * k : DEPTH * (k + 1), :] = get(slice(rows - DEPTH, rows), slice(0, flat))
        y_lo[k] = get(slice(0, rows), slice(0, yw))
        y_hi[k] = get(slice(0, rows), slice(flat - yw, flat))


def _messages(saved_pops, seed, solid, mask, field):
    steps = saved_pops.shape[0]
    _, rows, flat = seed.shape
    nfield = 19 + 3 * (steps - 1) + 2
    yw = DEPTH * NZ
    shapes = [(nfield * DEPTH, flat), (nfield * DEPTH, flat), (nfield, rows, yw), (nfield, rows, yw)]
    args = [saved_pops, seed, solid, mask, field]

    def full(shape):
        nd = len(shape)
        return pl.BlockSpec(shape, lambda i, _n=nd: (0,) * _n)

    return pl.pallas_call(
        _prep_kernel,
        grid=(1,),
        in_specs=[full(a.shape) for a in args],
        out_specs=[full(sh) for sh in shapes],
        out_shape=[jax.ShapeDtypeStruct(sh, jnp.float32) for sh in shapes],
        scratch_shapes=[pltpu.VMEM((3 * (steps - 1), rows, flat), jnp.float32)],
    )(*args)


def _shift(n, d):
    return [(i, (i + d) % n) for i in range(n)]


def body(saved_pops, seed_adjoint, solid_label, design_mask, design_field):
    nx = lax.axis_size("gx")
    ny = lax.axis_size("gy")
    _, rows, flat = seed_adjoint.shape
    yw = DEPTH * NZ
    lo_l, hi_l = slice(0, yw), slice(flat - yw, flat)
    x_lo, x_hi, y_lo, y_hi = _messages(saved_pops, seed_adjoint, solid_label, design_mask, design_field)
    hxp = lax.ppermute(x_lo, "gx", _shift(nx, -1))
    hxm = lax.ppermute(x_hi, "gx", _shift(nx, 1))
    hyp = lax.ppermute(y_lo, "gy", _shift(ny, -1))
    hym = lax.ppermute(y_hi, "gy", _shift(ny, 1))
    nfield = y_lo.shape[0]
    xp3 = hxp.reshape(nfield, DEPTH, flat)
    xm3 = hxm.reshape(nfield, DEPTH, flat)
    c_lo = jnp.concatenate([xp3[:, :, lo_l], xm3[:, :, lo_l]], axis=1).reshape(-1, yw)
    c_hi = jnp.concatenate([xp3[:, :, hi_l], xm3[:, :, hi_l]], axis=1).reshape(-1, yw)
    cp = lax.ppermute(c_lo, "gy", _shift(ny, -1))
    cm = lax.ppermute(c_hi, "gy", _shift(ny, 1))
    erows = rows + 2 * DEPTH
    eflat = flat + 2 * yw
    ext = (19, erows, eflat)
    args = [saved_pops, seed_adjoint, solid_label, design_mask, design_field, hxp, hxm, hyp, hym, cp, cm]

    def full(shape):
        nd = len(shape)
        return pl.BlockSpec(shape, lambda i, _n=nd: (0,) * _n)

    adjoint, sensitivity = pl.pallas_call(
        _fused_kernel,
        grid=(1,),
        in_specs=[full(a.shape) for a in args],
        out_specs=[full(seed_adjoint.shape), full((rows, flat))],
        out_shape=[
            jax.ShapeDtypeStruct(seed_adjoint.shape, jnp.float32),
            jax.ShapeDtypeStruct((rows, flat), jnp.float32),
        ],
        scratch_shapes=[
            pltpu.VMEM(ext, jnp.float32),
            pltpu.VMEM(ext, jnp.float32),
            pltpu.VMEM((3, erows, eflat), jnp.float32),
            pltpu.VMEM((erows, eflat), jnp.float32),
            pltpu.VMEM((erows, eflat), jnp.float32),
        ],
    )(*args)
    return (adjoint, sensitivity)


def solution(mesh):
    in_specs = (
        P(None, None, "gx", "gy"),
        P(None, "gx", "gy"),
        P("gx", "gy"),
        P("gx", "gy"),
        P("gx", "gy"),
    )
    out_specs = (P(None, "gx", "gy"), P("gx", "gy"))
    return jax.shard_map(body, mesh=mesh, in_specs=in_specs, out_specs=out_specs, check_vma=False)
```

```python
import jax
import jax.numpy as jnp
import numpy as np
from jax import lax
from jax.experimental import pallas as pl
from jax.experimental.pallas import tpu as pltpu
from jax.sharding import PartitionSpec as P

NZ = 32


VELOCITIES = np.array(
    [
        [0, 0, 0],
        [1, 0, 0],
        [-1, 0, 0],
        [0, 1, 0],
        [0, -1, 0],
        [0, 0, 1],
        [0, 0, -1],
        [1, 1, 0],
        [1, -1, 0],
        [-1, 1, 0],
        [-1, -1, 0],
        [1, 0, 1],
        [1, 0, -1],
        [-1, 0, 1],
        [-1, 0, -1],
        [0, 1, 1],
        [0, 1, -1],
        [0, -1, 1],
        [0, -1, -1],
    ]
)
LATTICE_WEIGHTS = np.array([1.0 / 3.0] + [1.0 / 18.0] * 6 + [1.0 / 36.0] * 12)
OPPOSITE = np.array([0, 2, 1, 4, 3, 6, 5, 10, 9, 8, 7, 14, 13, 12, 11, 18, 17, 16, 15])
OMEGA_BASE = 1.0
OMEGA_SPAN = 0.8
SENS_SCALE = 10.0

W32 = [float(np.float32(w)) for w in LATTICE_WEIGHTS]
XP = [i for i in range(19) if VELOCITIES[i, 0] == 1]
XM = [i for i in range(19) if VELOCITIES[i, 0] == -1]
YP = [i for i in range(19) if VELOCITIES[i, 1] == 1]
YM = [i for i in range(19) if VELOCITIES[i, 1] == -1]
LANES = 128


def _velocity(f):
    rho = f[0]
    for i in range(1, 19):
        rho = rho + f[i]
    mom = []
    for a in range(3):
        pos = [f[i] for i in range(19) if VELOCITIES[i, a] > 0]
        neg = [f[i] for i in range(19) if VELOCITIES[i, a] < 0]
        acc = pos[0]
        for x in pos[1:]:
            acc = acc + x
        for x in neg:
            acc = acc - x
        mom.append(acc)
    return rho, [m / rho for m in mom]


PAIRS = [(i, int(OPPOSITE[i])) for i in range(1, 19) if i < OPPOSITE[i]]


def _dot_c(i, vec):
    acc = None
    for a in range(3):
        c = int(VELOCITIES[i, a])
        if c == 0:
            continue
        if acc is None:
            acc = vec[a] if c > 0 else -vec[a]
        else:
            acc = acc + vec[a] if c > 0 else acc - vec[a]
    return acc


def _vjp_core(u, g, rate, solid):
    usq = u[0] * u[0] + u[1] * u[1] + u[2] * u[2]
    base = 1.0 - 1.5 * usq
    fluid = solid == 0
    gw = [g[i] * W32[i] for i in range(19)]
    e = [rate * x for x in gw]
    esum = e[0]
    easum = e[0] * base
    mb = [None, None, None]
    shape = []
    for i, j in PAIRS:
        p = _dot_c(i, u)
        p3 = 3.0 * p
        q = base + 1.5 * p * p3
        sm = e[i] + e[j]
        df = e[i] - e[j]
        esum = esum + sm
        easum = easum + (q * sm + p3 * df)
        ep = 3.0 * df + 3.0 * p3 * sm
        for a in range(3):
            c = int(VELOCITIES[i, a])
            if c == 0:
                continue
            if mb[a] is None:
                mb[a] = ep if c > 0 else -ep
            else:
                mb[a] = mb[a] + ep if c > 0 else mb[a] - ep
        shape.append((q, p3))
    mb = [mb[a] - 3.0 * u[a] * esum for a in range(3)]
    rhobar = easum - (mb[0] * u[0] + mb[1] * u[1] + mb[2] * u[2])
    one_minus = 1.0 - rate
    out = [None] * 19
    out[0] = jnp.where(fluid, one_minus * g[0] + rhobar, g[0])
    for i, j in PAIRS:
        k = _dot_c(i, mb)
        out[i] = jnp.where(fluid, one_minus * g[i] + (rhobar + k), g[j])
        out[j] = jnp.where(fluid, one_minus * g[j] + (rhobar - k), g[i])
    return out, shape, gw


def _collide_vjp(f, g, rate, solid):
    rho, u = _velocity(f)
    out, shape, gw = _vjp_core(u, g, rate, solid)
    gwa = gw[0] * (1.0 - 1.5 * (u[0] * u[0] + u[1] * u[1] + u[2] * u[2]))
    gf = g[0] * f[0]
    for (i, j), (q, p3) in zip(PAIRS, shape):
        gwa = gwa + (q * (gw[i] + gw[j]) + p3 * (gw[i] - gw[j]))
        gf = gf + (g[i] * f[i] + g[j] * f[j])
    rbar = rho * gwa - gf
    return out, rbar


DEPTH = 4


def _pull_all(a_ref, p_ref):
    _, rows, flat = a_ref.shape
    zl = lax.broadcasted_iota(jnp.int32, (rows, flat), 1) % NZ
    for i in range(19):
        cx, cy, cz = (int(c) for c in VELOCITIES[i])
        v = a_ref[i]
        if cx != 0:
            v = pltpu.roll(v, (rows - cx) % rows, 0)
        if cy != 0:
            v = pltpu.roll(v, (flat - cy * NZ) % flat, 1)
        if cz == 1:
            v = jnp.where(zl == NZ - 1, pltpu.roll(v, NZ - 1, 1), pltpu.roll(v, flat - 1, 1))
        elif cz == -1:
            v = jnp.where(zl == 0, pltpu.roll(v, flat - NZ + 1, 1), pltpu.roll(v, 1, 1))
        p_ref[i] = v


def _fill_ext(dst, own, hxp, hxm, hyp, hym, cp, cm, rows, flat):
    yw = DEPTH * NZ
    if own is not None:
        dst[0:rows, 0:flat] = own
    dst[rows : rows + DEPTH, 0:flat] = hxp
    dst[rows + DEPTH : rows + 2 * DEPTH, 0:flat] = hxm
    dst[0:rows, flat : flat + yw] = hyp
    dst[rows : rows + 2 * DEPTH, flat : flat + yw] = cp
    dst[0:rows, flat + yw : flat + 2 * yw] = hym
    dst[rows : rows + 2 * DEPTH, flat + yw : flat + 2 * yw] = cm


def _fused_kernel(pops_ref, seed_ref, solid_ref, mask_ref, field_ref, hxp, hxm, hyp, hym, cp, cm,
                  adj_out, sens_out, a_ref, p_ref, u_ref, rate_ref, solid_ext):
    steps = pops_ref.shape[0]
    _, rows, flat = seed_ref.shape
    erows, eflat = a_ref.shape[1], a_ref.shape[2]
    nfield = hyp.shape[0]
    mask_all = mask_ref[...].astype(jnp.float32)
    rate_own = OMEGA_BASE + OMEGA_SPAN * field_ref[...] * mask_all
    def halo(k, scale=None):
        parts = [
            hxp[DEPTH * k : DEPTH * (k + 1), :],
            hxm[DEPTH * k : DEPTH * (k + 1), :],
            hyp[k],
            hym[k],
            cp[2 * DEPTH * k : 2 * DEPTH * (k + 1), :],
            cm[2 * DEPTH * k : 2 * DEPTH * (k + 1), :],
        ]
        return parts if scale is None else [p * scale for p in parts]
    _fill_ext(rate_ref, rate_own, *halo(nfield - 2), rows, flat)
    _fill_ext(solid_ext, solid_ref[...].astype(jnp.float32), *halo(nfield - 1), rows, flat)
    for i in range(19):
        _fill_ext(a_ref.at[i], seed_ref[i], *halo(i), rows, flat)
    sens_out[...] = jnp.zeros(sens_out.shape, jnp.float32)
    row_tiles = rows // 8
    lane_tiles = flat // LANES
    ext_lane_tiles = eflat // LANES
    n_own = row_tiles * lane_tiles
    n_halo_rows = (erows - rows) // 8 * lane_tiles
    n_halo = n_halo_rows + (erows // 8) * (ext_lane_tiles - lane_tiles)

    def chunk(step, r0, l0, write_ref, own):
        rs = pl.ds(r0, 8)
        ls = pl.ds(l0, LANES)
        g = [p_ref[i, rs, ls] for i in range(19)]
        solid = solid_ext[rs, ls]
        solid_i = jnp.where(solid > 0.5, 1, 0)
        rate = rate_ref[rs, ls]
        if own:
            f = [pops_ref[step, i, rs, ls].astype(jnp.float32) * W32[i] for i in range(19)]
            new, rbar = _collide_vjp(f, g, rate, solid_i)
            mask = mask_ref[rs, ls].astype(jnp.float32)
            contrib = SENS_SCALE * OMEGA_SPAN * mask * jnp.where(solid_i == 0, rbar, 0.0)
            sens_out[rs, ls] = sens_out[rs, ls] + contrib
        else:
            u = [u_ref[a, rs, ls] for a in range(3)]
            new, _, _ = _vjp_core(u, g, rate, solid_i)
        for i in range(19):
            write_ref[i, rs, ls] = new[i]

    for n, step in enumerate(reversed(range(steps))):
        last = step == 0
        if not last:
            for a in range(3):
                _fill_ext(u_ref.at[a], None, *halo(19 + 3 * n + a), rows, flat)
        _pull_all(a_ref, p_ref)
        write_ref = adj_out if last else a_ref

        def own_body(c, carry, write_ref=write_ref):
            r0 = pl.multiple_of((c // lane_tiles) * 8, 8)
            l0 = pl.multiple_of((c % lane_tiles) * LANES, LANES)
            chunk(step, r0, l0, write_ref, True)
            return carry

        lax.fori_loop(0, n_own, own_body, 0)
        if not last:

            def halo_body(c, carry):
                c2 = c - n_halo_rows
                ext_w = ext_lane_tiles - lane_tiles
                r = jnp.where(c < n_halo_rows, rows // 8 + c // lane_tiles, c2 // ext_w)
                t = jnp.where(c < n_halo_rows, c % lane_tiles, lane_tiles + c2 % ext_w)
                chunk(step, pl.multiple_of(r * 8, 8), pl.multiple_of(t * LANES, LANES), a_ref, False)
                return carry

            lax.fori_loop(0, n_halo, halo_body, 0)


def _prep_kernel(pops_ref, seed_ref, solid_ref, mask_ref, field_ref, x_lo, x_hi, y_lo, y_hi, u_ref):
    steps = pops_ref.shape[0]
    _, rows, flat = seed_ref.shape
    yw = DEPTH * NZ
    for n, step in enumerate(reversed(range(1, steps))):
        for t in range(flat // LANES):
            sl = slice(LANES * t, LANES * (t + 1))
            f = [pops_ref[step, i, :, sl].astype(jnp.float32) * W32[i] for i in range(19)]
            _, u = _velocity(f)
            for a in range(3):
                u_ref[3 * n + a, :, sl] = u[a]
    nu = 3 * (steps - 1)
    rate = OMEGA_BASE + OMEGA_SPAN * field_ref[...] * mask_ref[...].astype(jnp.float32)
    solid = solid_ref[...].astype(jnp.float32)
    fields = [lambda rs, ls, i=i: seed_ref[i, rs, ls] for i in range(19)]
    fields += [lambda rs, ls, k=k: u_ref[k, rs, ls] for k in range(nu)]
    fields += [lambda rs, ls: rate[rs, ls], lambda rs, ls: solid[rs, ls]]
    for k, get in enumerate(fields):
        x_lo[DEPTH * k : DEPTH * (k + 1), :] = get(slice(0, DEPTH), slice(0, flat))
        x_hi[DEPTH * k : DEPTH * (k + 1), :] = get(slice(rows - DEPTH, rows), slice(0, flat))
        y_lo[k] = get(slice(0, rows), slice(0, yw))
        y_hi[k] = get(slice(0, rows), slice(flat - yw, flat))


def _messages(saved_pops, seed, solid, mask, field):
    steps = saved_pops.shape[0]
    _, rows, flat = seed.shape
    nfield = 19 + 3 * (steps - 1) + 2
    yw = DEPTH * NZ
    shapes = [(nfield * DEPTH, flat), (nfield * DEPTH, flat), (nfield, rows, yw), (nfield, rows, yw)]
    args = [saved_pops, seed, solid, mask, field]

    def full(shape):
        nd = len(shape)
        return pl.BlockSpec(shape, lambda i, _n=nd: (0,) * _n)

    return pl.pallas_call(
        _prep_kernel,
        grid=(1,),
        in_specs=[full(a.shape) for a in args],
        out_specs=[full(sh) for sh in shapes],
        out_shape=[jax.ShapeDtypeStruct(sh, jnp.float32) for sh in shapes],
        scratch_shapes=[pltpu.VMEM((3 * (steps - 1), rows, flat), jnp.float32)],
    )(*args)


def _shift(n, d):
    return [(i, (i + d) % n) for i in range(n)]


def body(saved_pops, seed_adjoint, solid_label, design_mask, design_field):
    nx = lax.axis_size("gx")
    ny = lax.axis_size("gy")
    _, rows, flat = seed_adjoint.shape
    yw = DEPTH * NZ
    lo_l, hi_l = slice(0, yw), slice(flat - yw, flat)
    x_lo, x_hi, y_lo, y_hi = _messages(saved_pops, seed_adjoint, solid_label, design_mask, design_field)
    hxp = lax.ppermute(x_lo, "gx", _shift(nx, -1))
    hxm = lax.ppermute(x_hi, "gx", _shift(nx, 1))
    hyp = lax.ppermute(y_lo, "gy", _shift(ny, -1))
    hym = lax.ppermute(y_hi, "gy", _shift(ny, 1))
    nfield = y_lo.shape[0]
    xp3 = hxp.reshape(nfield, DEPTH, flat)
    xm3 = hxm.reshape(nfield, DEPTH, flat)
    c_lo = jnp.concatenate([xp3[:, :, lo_l], xm3[:, :, lo_l]], axis=1).reshape(-1, yw)
    c_hi = jnp.concatenate([xp3[:, :, hi_l], xm3[:, :, hi_l]], axis=1).reshape(-1, yw)
    cp = lax.ppermute(c_lo, "gy", _shift(ny, -1))
    cm = lax.ppermute(c_hi, "gy", _shift(ny, 1))
    erows = rows + 2 * DEPTH
    eflat = flat + 2 * yw
    ext = (19, erows, eflat)
    args = [saved_pops, seed_adjoint, solid_label, design_mask, design_field, hxp, hxm, hyp, hym, cp, cm]

    def full(shape):
        nd = len(shape)
        return pl.BlockSpec(shape, lambda i, _n=nd: (0,) * _n)

    adjoint, sensitivity = pl.pallas_call(
        _fused_kernel,
        grid=(1,),
        in_specs=[full(a.shape) for a in args],
        out_specs=[full(seed_adjoint.shape), full((rows, flat))],
        out_shape=[
            jax.ShapeDtypeStruct(seed_adjoint.shape, jnp.float32),
            jax.ShapeDtypeStruct((rows, flat), jnp.float32),
        ],
        scratch_shapes=[
            pltpu.VMEM(ext, jnp.float32),
            pltpu.VMEM(ext, jnp.float32),
            pltpu.VMEM((3, erows, eflat), jnp.float32),
            pltpu.VMEM((erows, eflat), jnp.float32),
            pltpu.VMEM((erows, eflat), jnp.float32),
        ],
    )(*args)
    return (adjoint, sensitivity)


def solution(mesh):
    in_specs = (
        P(None, None, "gx", "gy"),
        P(None, "gx", "gy"),
        P("gx", "gy"),
        P("gx", "gy"),
        P("gx", "gy"),
    )
    out_specs = (P(None, "gx", "gy"), P("gx", "gy"))
    return jax.shard_map(body, mesh=mesh, in_specs=in_specs, out_specs=out_specs, check_vma=False)
```

```python
import jax
import jax.numpy as jnp
import numpy as np
from jax import lax
from jax.experimental import pallas as pl
from jax.experimental.pallas import tpu as pltpu
from jax.sharding import PartitionSpec as P

NZ = 32


VELOCITIES = np.array(
    [
        [0, 0, 0],
        [1, 0, 0],
        [-1, 0, 0],
        [0, 1, 0],
        [0, -1, 0],
        [0, 0, 1],
        [0, 0, -1],
        [1, 1, 0],
        [1, -1, 0],
        [-1, 1, 0],
        [-1, -1, 0],
        [1, 0, 1],
        [1, 0, -1],
        [-1, 0, 1],
        [-1, 0, -1],
        [0, 1, 1],
        [0, 1, -1],
        [0, -1, 1],
        [0, -1, -1],
    ]
)
LATTICE_WEIGHTS = np.array([1.0 / 3.0] + [1.0 / 18.0] * 6 + [1.0 / 36.0] * 12)
OPPOSITE = np.array([0, 2, 1, 4, 3, 6, 5, 10, 9, 8, 7, 14, 13, 12, 11, 18, 17, 16, 15])
OMEGA_BASE = 1.0
OMEGA_SPAN = 0.8
SENS_SCALE = 10.0

W32 = [float(np.float32(w)) for w in LATTICE_WEIGHTS]
XP = [i for i in range(19) if VELOCITIES[i, 0] == 1]
XM = [i for i in range(19) if VELOCITIES[i, 0] == -1]
YP = [i for i in range(19) if VELOCITIES[i, 1] == 1]
YM = [i for i in range(19) if VELOCITIES[i, 1] == -1]
LANES = 128


def _velocity(f):
    rho = f[0]
    for i in range(1, 19):
        rho = rho + f[i]
    mom = []
    for a in range(3):
        pos = [f[i] for i in range(19) if VELOCITIES[i, a] > 0]
        neg = [f[i] for i in range(19) if VELOCITIES[i, a] < 0]
        acc = pos[0]
        for x in pos[1:]:
            acc = acc + x
        for x in neg:
            acc = acc - x
        mom.append(acc)
    return rho, [m / rho for m in mom]


PAIRS = [(i, int(OPPOSITE[i])) for i in range(1, 19) if i < OPPOSITE[i]]


def _dot_c(i, vec):
    acc = None
    for a in range(3):
        c = int(VELOCITIES[i, a])
        if c == 0:
            continue
        if acc is None:
            acc = vec[a] if c > 0 else -vec[a]
        else:
            acc = acc + vec[a] if c > 0 else acc - vec[a]
    return acc


def _vjp_core(u, g, rate, solid):
    usq = u[0] * u[0] + u[1] * u[1] + u[2] * u[2]
    base = 1.0 - 1.5 * usq
    fluid = solid == 0
    gw = [g[i] * W32[i] for i in range(19)]
    e = [rate * x for x in gw]
    esum = e[0]
    easum = e[0] * base
    mb = [None, None, None]
    shape = []
    for i, j in PAIRS:
        p = _dot_c(i, u)
        p3 = 3.0 * p
        q = base + 1.5 * p * p3
        sm = e[i] + e[j]
        df = e[i] - e[j]
        esum = esum + sm
        easum = easum + (q * sm + p3 * df)
        ep = 3.0 * df + 3.0 * p3 * sm
        for a in range(3):
            c = int(VELOCITIES[i, a])
            if c == 0:
                continue
            if mb[a] is None:
                mb[a] = ep if c > 0 else -ep
            else:
                mb[a] = mb[a] + ep if c > 0 else mb[a] - ep
        shape.append((q, p3))
    mb = [mb[a] - 3.0 * u[a] * esum for a in range(3)]
    rhobar = easum - (mb[0] * u[0] + mb[1] * u[1] + mb[2] * u[2])
    one_minus = 1.0 - rate
    out = [None] * 19
    out[0] = jnp.where(fluid, one_minus * g[0] + rhobar, g[0])
    for i, j in PAIRS:
        k = _dot_c(i, mb)
        out[i] = jnp.where(fluid, one_minus * g[i] + (rhobar + k), g[j])
        out[j] = jnp.where(fluid, one_minus * g[j] + (rhobar - k), g[i])
    return out, shape, gw


def _collide_vjp(f, g, rate, solid):
    rho, u = _velocity(f)
    out, shape, gw = _vjp_core(u, g, rate, solid)
    gwa = gw[0] * (1.0 - 1.5 * (u[0] * u[0] + u[1] * u[1] + u[2] * u[2]))
    gf = g[0] * f[0]
    for (i, j), (q, p3) in zip(PAIRS, shape):
        gwa = gwa + (q * (gw[i] + gw[j]) + p3 * (gw[i] - gw[j]))
        gf = gf + (g[i] * f[i] + g[j] * f[j])
    rbar = rho * gwa - gf
    return out, rbar


DEPTH = 4


def _pull_all(a_ref, p_ref):
    _, rows, flat = a_ref.shape
    zl = lax.broadcasted_iota(jnp.int32, (rows, flat), 1) % NZ
    for i in range(19):
        cx, cy, cz = (int(c) for c in VELOCITIES[i])
        v = a_ref[i]
        if cx != 0:
            v = pltpu.roll(v, (rows - cx) % rows, 0)
        main = -(cy * NZ + cz) % flat
        if cz == 0:
            if main:
                v = pltpu.roll(v, main, 1)
        else:
            wrap = -(cy * NZ + cz - cz * NZ) % flat
            edge = NZ - 1 if cz == 1 else 0
            v = jnp.where(zl == edge, pltpu.roll(v, wrap, 1), pltpu.roll(v, main, 1))
        p_ref[i] = v


def _fill_ext(dst, own, hxp, hxm, hyp, hym, cp, cm, rows, flat):
    yw = DEPTH * NZ
    if own is not None:
        dst[0:rows, 0:flat] = own
    dst[rows : rows + DEPTH, 0:flat] = hxp
    dst[rows + DEPTH : rows + 2 * DEPTH, 0:flat] = hxm
    dst[0:rows, flat : flat + yw] = hyp
    dst[rows : rows + 2 * DEPTH, flat : flat + yw] = cp
    dst[0:rows, flat + yw : flat + 2 * yw] = hym
    dst[rows : rows + 2 * DEPTH, flat + yw : flat + 2 * yw] = cm


def _fused_kernel(pops_ref, seed_ref, solid_ref, mask_ref, field_ref, hxp, hxm, hyp, hym, cp, cm,
                  adj_out, sens_out, a_ref, p_ref, u_ref, rate_ref, solid_ext):
    steps = pops_ref.shape[0]
    _, rows, flat = seed_ref.shape
    erows, eflat = a_ref.shape[1], a_ref.shape[2]
    nfield = hyp.shape[0]
    mask_all = mask_ref[...].astype(jnp.float32)
    rate_own = OMEGA_BASE + OMEGA_SPAN * field_ref[...] * mask_all
    def halo(k, scale=None):
        parts = [
            hxp[DEPTH * k : DEPTH * (k + 1), :],
            hxm[DEPTH * k : DEPTH * (k + 1), :],
            hyp[k],
            hym[k],
            cp[2 * DEPTH * k : 2 * DEPTH * (k + 1), :],
            cm[2 * DEPTH * k : 2 * DEPTH * (k + 1), :],
        ]
        return parts if scale is None else [p * scale for p in parts]
    _fill_ext(rate_ref, rate_own, *halo(nfield - 2), rows, flat)
    _fill_ext(solid_ext, solid_ref[...].astype(jnp.float32), *halo(nfield - 1), rows, flat)
    for i in range(19):
        _fill_ext(a_ref.at[i], seed_ref[i], *halo(i), rows, flat)
    sens_out[...] = jnp.zeros(sens_out.shape, jnp.float32)
    row_tiles = rows // 8
    lane_tiles = flat // LANES
    ext_lane_tiles = eflat // LANES
    n_own = row_tiles * lane_tiles
    n_halo_rows = (erows - rows) // 8 * lane_tiles
    n_halo = n_halo_rows + (erows // 8) * (ext_lane_tiles - lane_tiles)

    def chunk(step, r0, l0, write_ref, own):
        rs = pl.ds(r0, 8)
        ls = pl.ds(l0, LANES)
        g = [p_ref[i, rs, ls] for i in range(19)]
        solid = solid_ext[rs, ls]
        solid_i = jnp.where(solid > 0.5, 1, 0)
        rate = rate_ref[rs, ls]
        if own:
            f = [pops_ref[step, i, rs, ls].astype(jnp.float32) * W32[i] for i in range(19)]
            new, rbar = _collide_vjp(f, g, rate, solid_i)
            mask = mask_ref[rs, ls].astype(jnp.float32)
            contrib = SENS_SCALE * OMEGA_SPAN * mask * jnp.where(solid_i == 0, rbar, 0.0)
            sens_out[rs, ls] = sens_out[rs, ls] + contrib
        else:
            u = [u_ref[a, rs, ls] for a in range(3)]
            new, _, _ = _vjp_core(u, g, rate, solid_i)
        for i in range(19):
            write_ref[i, rs, ls] = new[i]

    for n, step in enumerate(reversed(range(steps))):
        last = step == 0
        if not last:
            for a in range(3):
                _fill_ext(u_ref.at[a], None, *halo(19 + 3 * n + a), rows, flat)
        _pull_all(a_ref, p_ref)
        write_ref = adj_out if last else a_ref

        def own_body(c, carry, write_ref=write_ref):
            r0 = pl.multiple_of((c // lane_tiles) * 8, 8)
            l0 = pl.multiple_of((c % lane_tiles) * LANES, LANES)
            chunk(step, r0, l0, write_ref, True)
            return carry

        lax.fori_loop(0, n_own, own_body, 0)
        if not last:

            def halo_body(c, carry):
                c2 = c - n_halo_rows
                ext_w = ext_lane_tiles - lane_tiles
                r = jnp.where(c < n_halo_rows, rows // 8 + c // lane_tiles, c2 // ext_w)
                t = jnp.where(c < n_halo_rows, c % lane_tiles, lane_tiles + c2 % ext_w)
                chunk(step, pl.multiple_of(r * 8, 8), pl.multiple_of(t * LANES, LANES), a_ref, False)
                return carry

            lax.fori_loop(0, n_halo, halo_body, 0)


def _prep_kernel(pops_ref, seed_ref, solid_ref, mask_ref, field_ref, x_lo, x_hi, y_lo, y_hi, u_ref):
    steps = pops_ref.shape[0]
    _, rows, flat = seed_ref.shape
    yw = DEPTH * NZ
    for n, step in enumerate(reversed(range(1, steps))):
        for t in range(flat // LANES):
            sl = slice(LANES * t, LANES * (t + 1))
            f = [pops_ref[step, i, :, sl].astype(jnp.float32) * W32[i] for i in range(19)]
            _, u = _velocity(f)
            for a in range(3):
                u_ref[3 * n + a, :, sl] = u[a]
    nu = 3 * (steps - 1)
    rate = OMEGA_BASE + OMEGA_SPAN * field_ref[...] * mask_ref[...].astype(jnp.float32)
    solid = solid_ref[...].astype(jnp.float32)
    fields = [lambda rs, ls, i=i: seed_ref[i, rs, ls] for i in range(19)]
    fields += [lambda rs, ls, k=k: u_ref[k, rs, ls] for k in range(nu)]
    fields += [lambda rs, ls: rate[rs, ls], lambda rs, ls: solid[rs, ls]]
    for k, get in enumerate(fields):
        x_lo[DEPTH * k : DEPTH * (k + 1), :] = get(slice(0, DEPTH), slice(0, flat))
        x_hi[DEPTH * k : DEPTH * (k + 1), :] = get(slice(rows - DEPTH, rows), slice(0, flat))
        y_lo[k] = get(slice(0, rows), slice(0, yw))
        y_hi[k] = get(slice(0, rows), slice(flat - yw, flat))


def _messages(saved_pops, seed, solid, mask, field):
    steps = saved_pops.shape[0]
    _, rows, flat = seed.shape
    nfield = 19 + 3 * (steps - 1) + 2
    yw = DEPTH * NZ
    shapes = [(nfield * DEPTH, flat), (nfield * DEPTH, flat), (nfield, rows, yw), (nfield, rows, yw)]
    args = [saved_pops, seed, solid, mask, field]

    def full(shape):
        nd = len(shape)
        return pl.BlockSpec(shape, lambda i, _n=nd: (0,) * _n)

    return pl.pallas_call(
        _prep_kernel,
        grid=(1,),
        in_specs=[full(a.shape) for a in args],
        out_specs=[full(sh) for sh in shapes],
        out_shape=[jax.ShapeDtypeStruct(sh, jnp.float32) for sh in shapes],
        scratch_shapes=[pltpu.VMEM((3 * (steps - 1), rows, flat), jnp.float32)],
    )(*args)


def _shift(n, d):
    return [(i, (i + d) % n) for i in range(n)]


def body(saved_pops, seed_adjoint, solid_label, design_mask, design_field):
    nx = lax.axis_size("gx")
    ny = lax.axis_size("gy")
    _, rows, flat = seed_adjoint.shape
    yw = DEPTH * NZ
    lo_l, hi_l = slice(0, yw), slice(flat - yw, flat)
    x_lo, x_hi, y_lo, y_hi = _messages(saved_pops, seed_adjoint, solid_label, design_mask, design_field)
    hxp = lax.ppermute(x_lo, "gx", _shift(nx, -1))
    hxm = lax.ppermute(x_hi, "gx", _shift(nx, 1))
    hyp = lax.ppermute(y_lo, "gy", _shift(ny, -1))
    hym = lax.ppermute(y_hi, "gy", _shift(ny, 1))
    nfield = y_lo.shape[0]
    xp3 = hxp.reshape(nfield, DEPTH, flat)
    xm3 = hxm.reshape(nfield, DEPTH, flat)
    c_lo = jnp.concatenate([xp3[:, :, lo_l], xm3[:, :, lo_l]], axis=1).reshape(-1, yw)
    c_hi = jnp.concatenate([xp3[:, :, hi_l], xm3[:, :, hi_l]], axis=1).reshape(-1, yw)
    cp = lax.ppermute(c_lo, "gy", _shift(ny, -1))
    cm = lax.ppermute(c_hi, "gy", _shift(ny, 1))
    erows = rows + 2 * DEPTH
    eflat = flat + 2 * yw
    ext = (19, erows, eflat)
    args = [saved_pops, seed_adjoint, solid_label, design_mask, design_field, hxp, hxm, hyp, hym, cp, cm]

    def full(shape):
        nd = len(shape)
        return pl.BlockSpec(shape, lambda i, _n=nd: (0,) * _n)

    adjoint, sensitivity = pl.pallas_call(
        _fused_kernel,
        grid=(1,),
        in_specs=[full(a.shape) for a in args],
        out_specs=[full(seed_adjoint.shape), full((rows, flat))],
        out_shape=[
            jax.ShapeDtypeStruct(seed_adjoint.shape, jnp.float32),
            jax.ShapeDtypeStruct((rows, flat), jnp.float32),
        ],
        scratch_shapes=[
            pltpu.VMEM(ext, jnp.float32),
            pltpu.VMEM(ext, jnp.float32),
            pltpu.VMEM((3, erows, eflat), jnp.float32),
            pltpu.VMEM((erows, eflat), jnp.float32),
            pltpu.VMEM((erows, eflat), jnp.float32),
        ],
    )(*args)
    return (adjoint, sensitivity)


def solution(mesh):
    in_specs = (
        P(None, None, "gx", "gy"),
        P(None, "gx", "gy"),
        P("gx", "gy"),
        P("gx", "gy"),
        P("gx", "gy"),
    )
    out_specs = (P(None, "gx", "gy"), P("gx", "gy"))
    return jax.shard_map(body, mesh=mesh, in_specs=in_specs, out_specs=out_specs, check_vma=False)
```

```python
import jax
import jax.numpy as jnp
import numpy as np
from jax import lax
from jax.experimental import pallas as pl
from jax.experimental.pallas import tpu as pltpu
from jax.sharding import PartitionSpec as P

NZ = 32


VELOCITIES = np.array(
    [
        [0, 0, 0],
        [1, 0, 0],
        [-1, 0, 0],
        [0, 1, 0],
        [0, -1, 0],
        [0, 0, 1],
        [0, 0, -1],
        [1, 1, 0],
        [1, -1, 0],
        [-1, 1, 0],
        [-1, -1, 0],
        [1, 0, 1],
        [1, 0, -1],
        [-1, 0, 1],
        [-1, 0, -1],
        [0, 1, 1],
        [0, 1, -1],
        [0, -1, 1],
        [0, -1, -1],
    ]
)
LATTICE_WEIGHTS = np.array([1.0 / 3.0] + [1.0 / 18.0] * 6 + [1.0 / 36.0] * 12)
OPPOSITE = np.array([0, 2, 1, 4, 3, 6, 5, 10, 9, 8, 7, 14, 13, 12, 11, 18, 17, 16, 15])
OMEGA_BASE = 1.0
OMEGA_SPAN = 0.8
SENS_SCALE = 10.0

W32 = [float(np.float32(w)) for w in LATTICE_WEIGHTS]
XP = [i for i in range(19) if VELOCITIES[i, 0] == 1]
XM = [i for i in range(19) if VELOCITIES[i, 0] == -1]
YP = [i for i in range(19) if VELOCITIES[i, 1] == 1]
YM = [i for i in range(19) if VELOCITIES[i, 1] == -1]
LANES = 128


def _velocity(f):
    rho = f[0]
    for i in range(1, 19):
        rho = rho + f[i]
    mom = []
    for a in range(3):
        pos = [f[i] for i in range(19) if VELOCITIES[i, a] > 0]
        neg = [f[i] for i in range(19) if VELOCITIES[i, a] < 0]
        acc = pos[0]
        for x in pos[1:]:
            acc = acc + x
        for x in neg:
            acc = acc - x
        mom.append(acc)
    return rho, [m / rho for m in mom]


PAIRS = [(i, int(OPPOSITE[i])) for i in range(1, 19) if i < OPPOSITE[i]]


def _dot_c(i, vec):
    acc = None
    for a in range(3):
        c = int(VELOCITIES[i, a])
        if c == 0:
            continue
        if acc is None:
            acc = vec[a] if c > 0 else -vec[a]
        else:
            acc = acc + vec[a] if c > 0 else acc - vec[a]
    return acc


def _vjp_core(u, g, rate, solid):
    usq = u[0] * u[0] + u[1] * u[1] + u[2] * u[2]
    base = 1.0 - 1.5 * usq
    fluid = solid == 0
    gw = [g[i] * W32[i] for i in range(19)]
    e = [rate * x for x in gw]
    esum = e[0]
    easum = e[0] * base
    mb = [None, None, None]
    shape = []
    for i, j in PAIRS:
        p = _dot_c(i, u)
        p3 = 3.0 * p
        q = base + 1.5 * p * p3
        sm = e[i] + e[j]
        df = e[i] - e[j]
        esum = esum + sm
        easum = easum + (q * sm + p3 * df)
        ep = 3.0 * df + 3.0 * p3 * sm
        for a in range(3):
            c = int(VELOCITIES[i, a])
            if c == 0:
                continue
            if mb[a] is None:
                mb[a] = ep if c > 0 else -ep
            else:
                mb[a] = mb[a] + ep if c > 0 else mb[a] - ep
        shape.append((q, p3))
    mb = [mb[a] - 3.0 * u[a] * esum for a in range(3)]
    rhobar = easum - (mb[0] * u[0] + mb[1] * u[1] + mb[2] * u[2])
    one_minus = 1.0 - rate
    out = [None] * 19
    out[0] = jnp.where(fluid, one_minus * g[0] + rhobar, g[0])
    for i, j in PAIRS:
        k = _dot_c(i, mb)
        out[i] = jnp.where(fluid, one_minus * g[i] + (rhobar + k), g[j])
        out[j] = jnp.where(fluid, one_minus * g[j] + (rhobar - k), g[i])
    return out, shape, gw


def _collide_vjp(f, g, rate, solid):
    rho, u = _velocity(f)
    out, shape, gw = _vjp_core(u, g, rate, solid)
    gwa = gw[0] * (1.0 - 1.5 * (u[0] * u[0] + u[1] * u[1] + u[2] * u[2]))
    gf = g[0] * f[0]
    for (i, j), (q, p3) in zip(PAIRS, shape):
        gwa = gwa + (q * (gw[i] + gw[j]) + p3 * (gw[i] - gw[j]))
        gf = gf + (g[i] * f[i] + g[j] * f[j])
    rbar = rho * gwa - gf
    return out, rbar


DEPTH = 4


def _pull_all(a_ref, p_ref):
    _, rows, flat = a_ref.shape
    zl = lax.broadcasted_iota(jnp.int32, (rows, flat), 1) % NZ
    for i in range(19):
        cx, cy, cz = (int(c) for c in VELOCITIES[i])
        v = a_ref[i]
        if cx != 0:
            v = pltpu.roll(v, (rows - cx) % rows, 0)
        main = -(cy * NZ + cz) % flat
        if cz == 0:
            if main:
                v = pltpu.roll(v, main, 1)
        else:
            wrap = -(cy * NZ + cz - cz * NZ) % flat
            edge = NZ - 1 if cz == 1 else 0
            v = jnp.where(zl == edge, pltpu.roll(v, wrap, 1), pltpu.roll(v, main, 1))
        p_ref[i] = v


def _fill_ext(dst, own, hxp, hxm, hyp, hym, cp, cm, rows, flat):
    yw = DEPTH * NZ
    if own is not None:
        dst[0:rows, 0:flat] = own
    dst[rows : rows + DEPTH, 0:flat] = hxp
    dst[rows + DEPTH : rows + 2 * DEPTH, 0:flat] = hxm
    dst[0:rows, flat : flat + yw] = hyp
    dst[rows : rows + 2 * DEPTH, flat : flat + yw] = cp
    dst[0:rows, flat + yw : flat + 2 * yw] = hym
    dst[rows : rows + 2 * DEPTH, flat + yw : flat + 2 * yw] = cm


def _fused_kernel(pops_ref, seed_ref, solid_ref, mask_ref, field_ref, hxp, hxm, hyp, hym, cp, cm,
                  adj_out, sens_out, a_ref, p_ref, u_ref, rate_ref, solid_ext):
    steps = pops_ref.shape[0]
    _, rows, flat = seed_ref.shape
    erows, eflat = a_ref.shape[1], a_ref.shape[2]
    nfield = hyp.shape[0]
    mask_all = mask_ref[...].astype(jnp.float32)
    rate_own = OMEGA_BASE + OMEGA_SPAN * field_ref[...] * mask_all
    def halo(k, scale=None):
        parts = [
            hxp[DEPTH * k : DEPTH * (k + 1), :],
            hxm[DEPTH * k : DEPTH * (k + 1), :],
            hyp[k],
            hym[k],
            cp[2 * DEPTH * k : 2 * DEPTH * (k + 1), :],
            cm[2 * DEPTH * k : 2 * DEPTH * (k + 1), :],
        ]
        return parts if scale is None else [p * scale for p in parts]
    _fill_ext(rate_ref, rate_own, *halo(nfield - 2), rows, flat)
    _fill_ext(solid_ext, solid_ref[...].astype(jnp.float32), *halo(nfield - 1), rows, flat)
    for i in range(19):
        _fill_ext(a_ref.at[i], seed_ref[i], *halo(i), rows, flat)
    sens_out[...] = jnp.zeros(sens_out.shape, jnp.float32)
    row_tiles = rows // 8
    lane_tiles = flat // LANES
    ext_lane_tiles = eflat // LANES
    n_own = row_tiles * lane_tiles
    n_halo_rows = (erows - rows) // 8 * lane_tiles
    n_halo = n_halo_rows + (erows // 8) * (ext_lane_tiles - lane_tiles)

    def chunk(step, r0, l0, write_ref, own):
        rs = pl.ds(r0, 8)
        ls = pl.ds(l0, LANES)
        g = [p_ref[i, rs, ls] for i in range(19)]
        solid = solid_ext[rs, ls]
        solid_i = jnp.where(solid > 0.5, 1, 0)
        rate = rate_ref[rs, ls]
        if own:
            f = [pops_ref[step, i, rs, ls].astype(jnp.float32) * W32[i] for i in range(19)]
            new, rbar = _collide_vjp(f, g, rate, solid_i)
            mask = mask_ref[rs, ls].astype(jnp.float32)
            contrib = SENS_SCALE * OMEGA_SPAN * mask * jnp.where(solid_i == 0, rbar, 0.0)
            sens_out[rs, ls] = sens_out[rs, ls] + contrib
        else:
            u = [u_ref[a, rs, ls] for a in range(3)]
            new, _, _ = _vjp_core(u, g, rate, solid_i)
        for i in range(19):
            write_ref[i, rs, ls] = new[i]

    for n, step in enumerate(reversed(range(steps))):
        last = step == 0
        if not last:
            for a in range(3):
                _fill_ext(u_ref.at[a], None, *halo(19 + 3 * n + a), rows, flat)
        _pull_all(a_ref, p_ref)
        write_ref = adj_out if last else a_ref

        def own_body(c, carry, write_ref=write_ref):
            r0 = pl.multiple_of((c // lane_tiles) * 8, 8)
            l0 = pl.multiple_of((c % lane_tiles) * LANES, LANES)
            chunk(step, r0, l0, write_ref, True)
            return carry

        lax.fori_loop(0, n_own, own_body, 0)
        if not last:

            def halo_body(c, carry):
                c2 = c - n_halo_rows
                ext_w = ext_lane_tiles - lane_tiles
                r = jnp.where(c < n_halo_rows, rows // 8 + c // lane_tiles, c2 // ext_w)
                t = jnp.where(c < n_halo_rows, c % lane_tiles, lane_tiles + c2 % ext_w)
                chunk(step, pl.multiple_of(r * 8, 8), pl.multiple_of(t * LANES, LANES), a_ref, False)
                return carry

            lax.fori_loop(0, n_halo, halo_body, 0)


def _prep_kernel(pops_ref, seed_ref, solid_ref, mask_ref, field_ref, x_lo, x_hi, y_lo, y_hi):
    nsteps = pl.num_programs(0)
    _, rows, flat = seed_ref.shape
    yw = DEPTH * NZ
    tiles = flat // LANES
    pid = pl.program_id(0)

    def put(k, val, sl, t):
        x_lo[DEPTH * k : DEPTH * (k + 1), sl] = val[0:DEPTH, :]
        x_hi[DEPTH * k : DEPTH * (k + 1), sl] = val[rows - DEPTH : rows, :]
        if t == 0:
            y_lo[k] = val[:, 0:yw]
        if t == tiles - 1:
            y_hi[k] = val[:, LANES - yw : LANES]

    @pl.when(pid == 0)
    def _():
        nfield = y_lo.shape[0]
        for t in range(tiles):
            sl = slice(LANES * t, LANES * (t + 1))
            mask = mask_ref[:, sl].astype(jnp.float32)
            rate = OMEGA_BASE + OMEGA_SPAN * field_ref[:, sl] * mask
            put(nfield - 2, rate, sl, t)
            put(nfield - 1, solid_ref[:, sl].astype(jnp.float32), sl, t)
            for i in range(19):
                put(i, seed_ref[i, :, sl], sl, t)

    for n in range((y_lo.shape[0] - 21) // 3):

        @pl.when(pid == n)
        def _(n=n):
            for t in range(tiles):
                sl = slice(LANES * t, LANES * (t + 1))
                f = [pops_ref[0, i, :, sl].astype(jnp.float32) * W32[i] for i in range(19)]
                _, u = _velocity(f)
                for a in range(3):
                    put(19 + 3 * n + a, u[a], sl, t)


def _messages(saved_pops, seed, solid, mask, field):
    steps = saved_pops.shape[0]
    _, rows, flat = seed.shape
    nfield = 19 + 3 * (steps - 1) + 2
    yw = DEPTH * NZ
    shapes = [(nfield * DEPTH, flat), (nfield * DEPTH, flat), (nfield, rows, yw), (nfield, rows, yw)]
    args = [saved_pops, seed, solid, mask, field]

    def full(shape):
        nd = len(shape)
        return pl.BlockSpec(shape, lambda n, _n=nd: (0,) * _n)

    pops_spec = pl.BlockSpec((1, 19, rows, flat), lambda n: (steps - 1 - n, 0, 0, 0))
    return pl.pallas_call(
        _prep_kernel,
        grid=(steps - 1,),
        in_specs=[pops_spec] + [full(a.shape) for a in args[1:]],
        out_specs=[full(sh) for sh in shapes],
        out_shape=[jax.ShapeDtypeStruct(sh, jnp.float32) for sh in shapes],
    )(*args)


def _shift(n, d):
    return [(i, (i + d) % n) for i in range(n)]


def body(saved_pops, seed_adjoint, solid_label, design_mask, design_field):
    nx = lax.axis_size("gx")
    ny = lax.axis_size("gy")
    _, rows, flat = seed_adjoint.shape
    yw = DEPTH * NZ
    lo_l, hi_l = slice(0, yw), slice(flat - yw, flat)
    x_lo, x_hi, y_lo, y_hi = _messages(saved_pops, seed_adjoint, solid_label, design_mask, design_field)
    hxp = lax.ppermute(x_lo, "gx", _shift(nx, -1))
    hxm = lax.ppermute(x_hi, "gx", _shift(nx, 1))
    hyp = lax.ppermute(y_lo, "gy", _shift(ny, -1))
    hym = lax.ppermute(y_hi, "gy", _shift(ny, 1))
    nfield = y_lo.shape[0]
    xp3 = hxp.reshape(nfield, DEPTH, flat)
    xm3 = hxm.reshape(nfield, DEPTH, flat)
    c_lo = jnp.concatenate([xp3[:, :, lo_l], xm3[:, :, lo_l]], axis=1).reshape(-1, yw)
    c_hi = jnp.concatenate([xp3[:, :, hi_l], xm3[:, :, hi_l]], axis=1).reshape(-1, yw)
    cp = lax.ppermute(c_lo, "gy", _shift(ny, -1))
    cm = lax.ppermute(c_hi, "gy", _shift(ny, 1))
    erows = rows + 2 * DEPTH
    eflat = flat + 2 * yw
    ext = (19, erows, eflat)
    args = [saved_pops, seed_adjoint, solid_label, design_mask, design_field, hxp, hxm, hyp, hym, cp, cm]

    def full(shape):
        nd = len(shape)
        return pl.BlockSpec(shape, lambda i, _n=nd: (0,) * _n)

    adjoint, sensitivity = pl.pallas_call(
        _fused_kernel,
        grid=(1,),
        in_specs=[full(a.shape) for a in args],
        out_specs=[full(seed_adjoint.shape), full((rows, flat))],
        out_shape=[
            jax.ShapeDtypeStruct(seed_adjoint.shape, jnp.float32),
            jax.ShapeDtypeStruct((rows, flat), jnp.float32),
        ],
        scratch_shapes=[
            pltpu.VMEM(ext, jnp.float32),
            pltpu.VMEM(ext, jnp.float32),
            pltpu.VMEM((3, erows, eflat), jnp.float32),
            pltpu.VMEM((erows, eflat), jnp.float32),
            pltpu.VMEM((erows, eflat), jnp.float32),
        ],
    )(*args)
    return (adjoint, sensitivity)


def solution(mesh):
    in_specs = (
        P(None, None, "gx", "gy"),
        P(None, "gx", "gy"),
        P("gx", "gy"),
        P("gx", "gy"),
        P("gx", "gy"),
    )
    out_specs = (P(None, "gx", "gy"), P("gx", "gy"))
    return jax.shard_map(body, mesh=mesh, in_specs=in_specs, out_specs=out_specs, check_vma=False)
```

```python
import jax
import jax.numpy as jnp
import numpy as np
from jax import lax
from jax.experimental import pallas as pl
from jax.experimental.pallas import tpu as pltpu
from jax.sharding import PartitionSpec as P

NZ = 32


VELOCITIES = np.array(
    [
        [0, 0, 0],
        [1, 0, 0],
        [-1, 0, 0],
        [0, 1, 0],
        [0, -1, 0],
        [0, 0, 1],
        [0, 0, -1],
        [1, 1, 0],
        [1, -1, 0],
        [-1, 1, 0],
        [-1, -1, 0],
        [1, 0, 1],
        [1, 0, -1],
        [-1, 0, 1],
        [-1, 0, -1],
        [0, 1, 1],
        [0, 1, -1],
        [0, -1, 1],
        [0, -1, -1],
    ]
)
LATTICE_WEIGHTS = np.array([1.0 / 3.0] + [1.0 / 18.0] * 6 + [1.0 / 36.0] * 12)
OPPOSITE = np.array([0, 2, 1, 4, 3, 6, 5, 10, 9, 8, 7, 14, 13, 12, 11, 18, 17, 16, 15])
OMEGA_BASE = 1.0
OMEGA_SPAN = 0.8
SENS_SCALE = 10.0

W32 = [float(np.float32(w)) for w in LATTICE_WEIGHTS]
XP = [i for i in range(19) if VELOCITIES[i, 0] == 1]
XM = [i for i in range(19) if VELOCITIES[i, 0] == -1]
YP = [i for i in range(19) if VELOCITIES[i, 1] == 1]
YM = [i for i in range(19) if VELOCITIES[i, 1] == -1]
LANES = 128


def _velocity(f):
    rho = f[0]
    for i in range(1, 19):
        rho = rho + f[i]
    mom = []
    for a in range(3):
        pos = [f[i] for i in range(19) if VELOCITIES[i, a] > 0]
        neg = [f[i] for i in range(19) if VELOCITIES[i, a] < 0]
        acc = pos[0]
        for x in pos[1:]:
            acc = acc + x
        for x in neg:
            acc = acc - x
        mom.append(acc)
    return rho, [m / rho for m in mom]


PAIRS = [(i, int(OPPOSITE[i])) for i in range(1, 19) if i < OPPOSITE[i]]


def _dot_c(i, vec):
    acc = None
    for a in range(3):
        c = int(VELOCITIES[i, a])
        if c == 0:
            continue
        if acc is None:
            acc = vec[a] if c > 0 else -vec[a]
        else:
            acc = acc + vec[a] if c > 0 else acc - vec[a]
    return acc


def _vjp_core(u, g, rate, solid):
    usq = u[0] * u[0] + u[1] * u[1] + u[2] * u[2]
    base = 1.0 - 1.5 * usq
    fluid = solid == 0
    gw = [g[i] * W32[i] for i in range(19)]
    e = [rate * x for x in gw]
    esum = e[0]
    easum = e[0] * base
    mb = [None, None, None]
    shape = []
    for i, j in PAIRS:
        p = _dot_c(i, u)
        p3 = 3.0 * p
        q = base + 1.5 * p * p3
        sm = e[i] + e[j]
        df = e[i] - e[j]
        esum = esum + sm
        easum = easum + (q * sm + p3 * df)
        ep = 3.0 * df + 3.0 * p3 * sm
        for a in range(3):
            c = int(VELOCITIES[i, a])
            if c == 0:
                continue
            if mb[a] is None:
                mb[a] = ep if c > 0 else -ep
            else:
                mb[a] = mb[a] + ep if c > 0 else mb[a] - ep
        shape.append((q, p3))
    mb = [mb[a] - 3.0 * u[a] * esum for a in range(3)]
    rhobar = easum - (mb[0] * u[0] + mb[1] * u[1] + mb[2] * u[2])
    one_minus = 1.0 - rate
    out = [None] * 19
    out[0] = jnp.where(fluid, one_minus * g[0] + rhobar, g[0])
    for i, j in PAIRS:
        k = _dot_c(i, mb)
        out[i] = jnp.where(fluid, one_minus * g[i] + (rhobar + k), g[j])
        out[j] = jnp.where(fluid, one_minus * g[j] + (rhobar - k), g[i])
    return out, shape, gw


def _collide_vjp(f, g, rate, solid):
    rho, u = _velocity(f)
    out, shape, gw = _vjp_core(u, g, rate, solid)
    gwa = gw[0] * (1.0 - 1.5 * (u[0] * u[0] + u[1] * u[1] + u[2] * u[2]))
    gf = g[0] * f[0]
    for (i, j), (q, p3) in zip(PAIRS, shape):
        gwa = gwa + (q * (gw[i] + gw[j]) + p3 * (gw[i] - gw[j]))
        gf = gf + (g[i] * f[i] + g[j] * f[j])
    rbar = rho * gwa - gf
    return out, rbar


DEPTH = 4


def _pull_all(a_ref, p_ref):
    _, rows, flat = a_ref.shape
    zl = lax.broadcasted_iota(jnp.int32, (rows, flat), 1) % NZ
    for i in range(19):
        cx, cy, cz = (int(c) for c in VELOCITIES[i])
        v = a_ref[i]
        if cx != 0:
            v = pltpu.roll(v, (rows - cx) % rows, 0)
        main = -(cy * NZ + cz) % flat
        if cz == 0:
            if main:
                v = pltpu.roll(v, main, 1)
        else:
            wrap = -(cy * NZ + cz - cz * NZ) % flat
            edge = NZ - 1 if cz == 1 else 0
            v = jnp.where(zl == edge, pltpu.roll(v, wrap, 1), pltpu.roll(v, main, 1))
        p_ref[i] = v


def _fill_ext(dst, own, hxp, hxm, hyp, hym, cp, cm, rows, flat):
    yw = DEPTH * NZ
    if own is not None:
        dst[0:rows, 0:flat] = own
    dst[rows : rows + DEPTH, 0:flat] = hxp
    dst[rows + DEPTH : rows + 2 * DEPTH, 0:flat] = hxm
    dst[0:rows, flat : flat + yw] = hyp
    dst[rows : rows + 2 * DEPTH, flat : flat + yw] = cp
    dst[0:rows, flat + yw : flat + 2 * yw] = hym
    dst[rows : rows + 2 * DEPTH, flat + yw : flat + 2 * yw] = cm


def _fused_kernel(pops_ref, seed_ref, solid_ref, mask_ref, field_ref, hxp, hxm, hyp, hym, cp, cm,
                  adj_out, sens_out, a_ref, p_ref, u_ref, rate_ref, solid_ext):
    steps = pops_ref.shape[0]
    _, rows, flat = seed_ref.shape
    erows, eflat = a_ref.shape[1], a_ref.shape[2]
    nfield = hyp.shape[0]
    mask_all = mask_ref[...].astype(jnp.float32)
    rate_own = OMEGA_BASE + OMEGA_SPAN * field_ref[...] * mask_all
    def halo(k, scale=None):
        parts = [
            hxp[DEPTH * k : DEPTH * (k + 1), :],
            hxm[DEPTH * k : DEPTH * (k + 1), :],
            hyp[k],
            hym[k],
            cp[2 * DEPTH * k : 2 * DEPTH * (k + 1), :],
            cm[2 * DEPTH * k : 2 * DEPTH * (k + 1), :],
        ]
        return parts if scale is None else [p * scale for p in parts]
    _fill_ext(rate_ref, rate_own, *halo(nfield - 2), rows, flat)
    _fill_ext(solid_ext, solid_ref[...].astype(jnp.float32), *halo(nfield - 1), rows, flat)
    for i in range(19):
        _fill_ext(a_ref.at[i], seed_ref[i], *halo(i), rows, flat)
    sens_out[...] = jnp.zeros(sens_out.shape, jnp.float32)
    row_tiles = rows // 8
    lane_tiles = flat // LANES
    ext_lane_tiles = eflat // LANES
    n_own = row_tiles * lane_tiles
    n_halo_rows = (erows - rows) // 8 * lane_tiles
    n_halo = n_halo_rows + (erows // 8) * (ext_lane_tiles - lane_tiles)

    def chunk(step, r0, l0, write_ref, own):
        rs = pl.ds(r0, 8)
        ls = pl.ds(l0, LANES)
        g = [p_ref[i, rs, ls] for i in range(19)]
        solid = solid_ext[rs, ls]
        solid_i = jnp.where(solid > 0.5, 1, 0)
        rate = rate_ref[rs, ls]
        if own:
            f = [pops_ref[step, i, rs, ls].astype(jnp.float32) * W32[i] for i in range(19)]
            new, rbar = _collide_vjp(f, g, rate, solid_i)
            mask = mask_ref[rs, ls].astype(jnp.float32)
            contrib = SENS_SCALE * OMEGA_SPAN * mask * jnp.where(solid_i == 0, rbar, 0.0)
            sens_out[rs, ls] = sens_out[rs, ls] + contrib
        else:
            u = [u_ref[a, rs, ls] for a in range(3)]
            new, _, _ = _vjp_core(u, g, rate, solid_i)
        for i in range(19):
            write_ref[i, rs, ls] = new[i]

    for n, step in enumerate(reversed(range(steps))):
        last = step == 0
        if not last:
            for a in range(3):
                _fill_ext(u_ref.at[a], None, *halo(19 + 3 * n + a), rows, flat)
        _pull_all(a_ref, p_ref)
        write_ref = adj_out if last else a_ref

        def own_body(c, carry, write_ref=write_ref):
            r0 = pl.multiple_of((c // lane_tiles) * 8, 8)
            l0 = pl.multiple_of((c % lane_tiles) * LANES, LANES)
            chunk(step, r0, l0, write_ref, True)
            return carry

        lax.fori_loop(0, n_own, own_body, 0, unroll=True)
        if not last:

            def halo_body(c, carry):
                c2 = c - n_halo_rows
                ext_w = ext_lane_tiles - lane_tiles
                r = jnp.where(c < n_halo_rows, rows // 8 + c // lane_tiles, c2 // ext_w)
                t = jnp.where(c < n_halo_rows, c % lane_tiles, lane_tiles + c2 % ext_w)
                chunk(step, pl.multiple_of(r * 8, 8), pl.multiple_of(t * LANES, LANES), a_ref, False)
                return carry

            lax.fori_loop(0, n_halo, halo_body, 0, unroll=True)


def _prep_kernel(pops_ref, seed_ref, solid_ref, mask_ref, field_ref, x_lo, x_hi, y_lo, y_hi, u_ref):
    steps = pops_ref.shape[0]
    _, rows, flat = seed_ref.shape
    yw = DEPTH * NZ
    for n, step in enumerate(reversed(range(1, steps))):
        for t in range(flat // LANES):
            sl = slice(LANES * t, LANES * (t + 1))
            f = [pops_ref[step, i, :, sl].astype(jnp.float32) * W32[i] for i in range(19)]
            _, u = _velocity(f)
            for a in range(3):
                u_ref[3 * n + a, :, sl] = u[a]
    nu = 3 * (steps - 1)
    rate = OMEGA_BASE + OMEGA_SPAN * field_ref[...] * mask_ref[...].astype(jnp.float32)
    solid = solid_ref[...].astype(jnp.float32)
    fields = [lambda rs, ls, i=i: seed_ref[i, rs, ls] for i in range(19)]
    fields += [lambda rs, ls, k=k: u_ref[k, rs, ls] for k in range(nu)]
    fields += [lambda rs, ls: rate[rs, ls], lambda rs, ls: solid[rs, ls]]
    for k, get in enumerate(fields):
        x_lo[DEPTH * k : DEPTH * (k + 1), :] = get(slice(0, DEPTH), slice(0, flat))
        x_hi[DEPTH * k : DEPTH * (k + 1), :] = get(slice(rows - DEPTH, rows), slice(0, flat))
        y_lo[k] = get(slice(0, rows), slice(0, yw))
        y_hi[k] = get(slice(0, rows), slice(flat - yw, flat))


def _messages(saved_pops, seed, solid, mask, field):
    steps = saved_pops.shape[0]
    _, rows, flat = seed.shape
    nfield = 19 + 3 * (steps - 1) + 2
    yw = DEPTH * NZ
    shapes = [(nfield * DEPTH, flat), (nfield * DEPTH, flat), (nfield, rows, yw), (nfield, rows, yw)]
    args = [saved_pops, seed, solid, mask, field]

    def full(shape):
        nd = len(shape)
        return pl.BlockSpec(shape, lambda i, _n=nd: (0,) * _n)

    return pl.pallas_call(
        _prep_kernel,
        grid=(1,),
        in_specs=[full(a.shape) for a in args],
        out_specs=[full(sh) for sh in shapes],
        out_shape=[jax.ShapeDtypeStruct(sh, jnp.float32) for sh in shapes],
        scratch_shapes=[pltpu.VMEM((3 * (steps - 1), rows, flat), jnp.float32)],
    )(*args)


def _shift(n, d):
    return [(i, (i + d) % n) for i in range(n)]


def body(saved_pops, seed_adjoint, solid_label, design_mask, design_field):
    nx = lax.axis_size("gx")
    ny = lax.axis_size("gy")
    _, rows, flat = seed_adjoint.shape
    yw = DEPTH * NZ
    lo_l, hi_l = slice(0, yw), slice(flat - yw, flat)
    x_lo, x_hi, y_lo, y_hi = _messages(saved_pops, seed_adjoint, solid_label, design_mask, design_field)
    hxp = lax.ppermute(x_lo, "gx", _shift(nx, -1))
    hxm = lax.ppermute(x_hi, "gx", _shift(nx, 1))
    hyp = lax.ppermute(y_lo, "gy", _shift(ny, -1))
    hym = lax.ppermute(y_hi, "gy", _shift(ny, 1))
    nfield = y_lo.shape[0]
    xp3 = hxp.reshape(nfield, DEPTH, flat)
    xm3 = hxm.reshape(nfield, DEPTH, flat)
    c_lo = jnp.concatenate([xp3[:, :, lo_l], xm3[:, :, lo_l]], axis=1).reshape(-1, yw)
    c_hi = jnp.concatenate([xp3[:, :, hi_l], xm3[:, :, hi_l]], axis=1).reshape(-1, yw)
    cp = lax.ppermute(c_lo, "gy", _shift(ny, -1))
    cm = lax.ppermute(c_hi, "gy", _shift(ny, 1))
    erows = rows + 2 * DEPTH
    eflat = flat + 2 * yw
    ext = (19, erows, eflat)
    args = [saved_pops, seed_adjoint, solid_label, design_mask, design_field, hxp, hxm, hyp, hym, cp, cm]

    def full(shape):
        nd = len(shape)
        return pl.BlockSpec(shape, lambda i, _n=nd: (0,) * _n)

    adjoint, sensitivity = pl.pallas_call(
        _fused_kernel,
        grid=(1,),
        in_specs=[full(a.shape) for a in args],
        out_specs=[full(seed_adjoint.shape), full((rows, flat))],
        out_shape=[
            jax.ShapeDtypeStruct(seed_adjoint.shape, jnp.float32),
            jax.ShapeDtypeStruct((rows, flat), jnp.float32),
        ],
        scratch_shapes=[
            pltpu.VMEM(ext, jnp.float32),
            pltpu.VMEM(ext, jnp.float32),
            pltpu.VMEM((3, erows, eflat), jnp.float32),
            pltpu.VMEM((erows, eflat), jnp.float32),
            pltpu.VMEM((erows, eflat), jnp.float32),
        ],
    )(*args)
    return (adjoint, sensitivity)


def solution(mesh):
    in_specs = (
        P(None, None, "gx", "gy"),
        P(None, "gx", "gy"),
        P("gx", "gy"),
        P("gx", "gy"),
        P("gx", "gy"),
    )
    out_specs = (P(None, "gx", "gy"), P("gx", "gy"))
    return jax.shard_map(body, mesh=mesh, in_specs=in_specs, out_specs=out_specs, check_vma=False)
```

```python
import jax
import jax.numpy as jnp
import numpy as np
from jax import lax
from jax.experimental import pallas as pl
from jax.experimental.pallas import tpu as pltpu
from jax.sharding import PartitionSpec as P

NZ = 32


VELOCITIES = np.array(
    [
        [0, 0, 0],
        [1, 0, 0],
        [-1, 0, 0],
        [0, 1, 0],
        [0, -1, 0],
        [0, 0, 1],
        [0, 0, -1],
        [1, 1, 0],
        [1, -1, 0],
        [-1, 1, 0],
        [-1, -1, 0],
        [1, 0, 1],
        [1, 0, -1],
        [-1, 0, 1],
        [-1, 0, -1],
        [0, 1, 1],
        [0, 1, -1],
        [0, -1, 1],
        [0, -1, -1],
    ]
)
LATTICE_WEIGHTS = np.array([1.0 / 3.0] + [1.0 / 18.0] * 6 + [1.0 / 36.0] * 12)
OPPOSITE = np.array([0, 2, 1, 4, 3, 6, 5, 10, 9, 8, 7, 14, 13, 12, 11, 18, 17, 16, 15])
OMEGA_BASE = 1.0
OMEGA_SPAN = 0.8
SENS_SCALE = 10.0

W32 = [float(np.float32(w)) for w in LATTICE_WEIGHTS]
XP = [i for i in range(19) if VELOCITIES[i, 0] == 1]
XM = [i for i in range(19) if VELOCITIES[i, 0] == -1]
YP = [i for i in range(19) if VELOCITIES[i, 1] == 1]
YM = [i for i in range(19) if VELOCITIES[i, 1] == -1]
LANES = 128


def _velocity(f):
    rho = f[0]
    for i in range(1, 19):
        rho = rho + f[i]
    mom = []
    for a in range(3):
        pos = [f[i] for i in range(19) if VELOCITIES[i, a] > 0]
        neg = [f[i] for i in range(19) if VELOCITIES[i, a] < 0]
        acc = pos[0]
        for x in pos[1:]:
            acc = acc + x
        for x in neg:
            acc = acc - x
        mom.append(acc)
    return rho, [m / rho for m in mom]


PAIRS = [(i, int(OPPOSITE[i])) for i in range(1, 19) if i < OPPOSITE[i]]


def _dot_c(i, vec):
    acc = None
    for a in range(3):
        c = int(VELOCITIES[i, a])
        if c == 0:
            continue
        if acc is None:
            acc = vec[a] if c > 0 else -vec[a]
        else:
            acc = acc + vec[a] if c > 0 else acc - vec[a]
    return acc


def _vjp_core(u, g, rate, solid):
    usq = u[0] * u[0] + u[1] * u[1] + u[2] * u[2]
    base = 1.0 - 1.5 * usq
    fluid = solid == 0
    gw = [g[i] * W32[i] for i in range(19)]
    e = [rate * x for x in gw]
    esum = e[0]
    easum = e[0] * base
    mb = [None, None, None]
    shape = []
    for i, j in PAIRS:
        p = _dot_c(i, u)
        p3 = 3.0 * p
        q = base + 1.5 * p * p3
        sm = e[i] + e[j]
        df = e[i] - e[j]
        esum = esum + sm
        easum = easum + (q * sm + p3 * df)
        ep = 3.0 * df + 3.0 * p3 * sm
        for a in range(3):
            c = int(VELOCITIES[i, a])
            if c == 0:
                continue
            if mb[a] is None:
                mb[a] = ep if c > 0 else -ep
            else:
                mb[a] = mb[a] + ep if c > 0 else mb[a] - ep
        shape.append((q, p3))
    mb = [mb[a] - 3.0 * u[a] * esum for a in range(3)]
    rhobar = easum - (mb[0] * u[0] + mb[1] * u[1] + mb[2] * u[2])
    one_minus = 1.0 - rate
    out = [None] * 19
    out[0] = jnp.where(fluid, one_minus * g[0] + rhobar, g[0])
    for i, j in PAIRS:
        k = _dot_c(i, mb)
        out[i] = jnp.where(fluid, one_minus * g[i] + (rhobar + k), g[j])
        out[j] = jnp.where(fluid, one_minus * g[j] + (rhobar - k), g[i])
    return out, shape, gw


def _collide_vjp(f, g, rate, solid):
    rho, u = _velocity(f)
    out, shape, gw = _vjp_core(u, g, rate, solid)
    gwa = gw[0] * (1.0 - 1.5 * (u[0] * u[0] + u[1] * u[1] + u[2] * u[2]))
    gf = g[0] * f[0]
    for (i, j), (q, p3) in zip(PAIRS, shape):
        gwa = gwa + (q * (gw[i] + gw[j]) + p3 * (gw[i] - gw[j]))
        gf = gf + (g[i] * f[i] + g[j] * f[j])
    rbar = rho * gwa - gf
    return out, rbar


DEPTH = 4


def _pull_all(a_ref, p_ref):
    _, rows, flat = a_ref.shape
    zl = lax.broadcasted_iota(jnp.int32, (rows, flat), 1) % NZ
    for i in range(19):
        cx, cy, cz = (int(c) for c in VELOCITIES[i])
        v = a_ref[i]
        if cx != 0:
            v = pltpu.roll(v, (rows - cx) % rows, 0)
        main = -(cy * NZ + cz) % flat
        if cz == 0:
            if main:
                v = pltpu.roll(v, main, 1)
        else:
            wrap = -(cy * NZ + cz - cz * NZ) % flat
            edge = NZ - 1 if cz == 1 else 0
            v = jnp.where(zl == edge, pltpu.roll(v, wrap, 1), pltpu.roll(v, main, 1))
        p_ref[i] = v


def _fill_ext(dst, own, hxp, hxm, hyp, hym, cp, cm, rows, flat):
    yw = DEPTH * NZ
    if own is not None:
        dst[0:rows, 0:flat] = own
    dst[rows : rows + DEPTH, 0:flat] = hxp
    dst[rows + DEPTH : rows + 2 * DEPTH, 0:flat] = hxm
    dst[0:rows, flat : flat + yw] = hyp
    dst[rows : rows + 2 * DEPTH, flat : flat + yw] = cp
    dst[0:rows, flat + yw : flat + 2 * yw] = hym
    dst[rows : rows + 2 * DEPTH, flat + yw : flat + 2 * yw] = cm


def _fused_kernel(pops_ref, seed_ref, solid_ref, mask_ref, field_ref, hxp, hxm, hyp, hym, cp, cm,
                  adj_out, sens_out, a_ref, p_ref, u_ref, rate_ref, solid_ext):
    steps = pops_ref.shape[0]
    _, rows, flat = seed_ref.shape
    erows, eflat = a_ref.shape[1], a_ref.shape[2]
    nfield = hyp.shape[0]
    mask_all = mask_ref[...].astype(jnp.float32)
    rate_own = OMEGA_BASE + OMEGA_SPAN * field_ref[...] * mask_all
    def halo(k, scale=None):
        parts = [
            hxp[DEPTH * k : DEPTH * (k + 1), :],
            hxm[DEPTH * k : DEPTH * (k + 1), :],
            hyp[k],
            hym[k],
            cp[2 * DEPTH * k : 2 * DEPTH * (k + 1), :],
            cm[2 * DEPTH * k : 2 * DEPTH * (k + 1), :],
        ]
        return parts if scale is None else [p * scale for p in parts]
    _fill_ext(rate_ref, rate_own, *halo(nfield - 2), rows, flat)
    _fill_ext(solid_ext, solid_ref[...].astype(jnp.float32), *halo(nfield - 1), rows, flat)
    for i in range(19):
        _fill_ext(a_ref.at[i], seed_ref[i], *halo(i), rows, flat)
    sens_out[...] = jnp.zeros(sens_out.shape, jnp.float32)
    row_tiles = rows // 8
    lane_tiles = flat // LANES
    ext_lane_tiles = eflat // LANES
    n_own = row_tiles * lane_tiles
    n_halo_rows = (erows - rows) // 8 * lane_tiles
    n_halo = n_halo_rows + (erows // 8) * (ext_lane_tiles - lane_tiles)

    def chunk(step, r0, l0, write_ref, own):
        rs = pl.ds(r0, 8)
        ls = pl.ds(l0, LANES)
        g = [p_ref[i, rs, ls] for i in range(19)]
        solid = solid_ext[rs, ls]
        solid_i = jnp.where(solid > 0.5, 1, 0)
        rate = rate_ref[rs, ls]
        if own:
            f = [pops_ref[step, i, rs, ls].astype(jnp.float32) * W32[i] for i in range(19)]
            new, rbar = _collide_vjp(f, g, rate, solid_i)
            mask = mask_ref[rs, ls].astype(jnp.float32)
            contrib = SENS_SCALE * OMEGA_SPAN * mask * jnp.where(solid_i == 0, rbar, 0.0)
            sens_out[rs, ls] = sens_out[rs, ls] + contrib
        else:
            u = [u_ref[a, rs, ls] for a in range(3)]
            new, _, _ = _vjp_core(u, g, rate, solid_i)
        for i in range(19):
            write_ref[i, rs, ls] = new[i]

    for n, step in enumerate(reversed(range(steps))):
        last = step == 0
        if not last:
            for a in range(3):
                _fill_ext(u_ref.at[a], None, *halo(19 + 3 * n + a), rows, flat)
        _pull_all(a_ref, p_ref)
        write_ref = adj_out if last else a_ref

        def own_body(c, carry, write_ref=write_ref):
            r0 = pl.multiple_of((c // lane_tiles) * 8, 8)
            l0 = pl.multiple_of((c % lane_tiles) * LANES, LANES)
            chunk(step, r0, l0, write_ref, True)
            return carry

        lax.fori_loop(0, n_own, own_body, 0, unroll=True)
        if not last:

            def halo_body(c, carry):
                c2 = c - n_halo_rows
                ext_w = ext_lane_tiles - lane_tiles
                r = jnp.where(c < n_halo_rows, rows // 8 + c // lane_tiles, c2 // ext_w)
                t = jnp.where(c < n_halo_rows, c % lane_tiles, lane_tiles + c2 % ext_w)
                chunk(step, pl.multiple_of(r * 8, 8), pl.multiple_of(t * LANES, LANES), a_ref, False)
                return carry

            lax.fori_loop(0, n_halo, halo_body, 0, unroll=True)


def _prep_kernel(pops_hbm, seed_ref, solid_ref, mask_ref, field_ref, x_lo, x_hi, y_lo, y_hi, u_ref,
                 pops_ref, sems):
    steps = pops_hbm.shape[0]
    _, rows, flat = seed_ref.shape
    yw = DEPTH * NZ
    copies = [
        pltpu.make_async_copy(pops_hbm.at[step], pops_ref.at[step - 1], sems.at[step - 1])
        for step in range(1, steps)
    ]
    for c in reversed(copies):
        c.start()
    rate = OMEGA_BASE + OMEGA_SPAN * field_ref[...] * mask_ref[...].astype(jnp.float32)
    solid = solid_ref[...].astype(jnp.float32)
    nu = 3 * (steps - 1)
    fields = {i: (lambda rs, ls, i=i: seed_ref[i, rs, ls]) for i in range(19)}
    fields[19 + nu] = lambda rs, ls: rate[rs, ls]
    fields[20 + nu] = lambda rs, ls: solid[rs, ls]
    _put_fields(fields, x_lo, x_hi, y_lo, y_hi, rows, flat)
    for n, step in enumerate(reversed(range(1, steps))):
        copies[step - 1].wait()
        for t in range(flat // LANES):
            sl = slice(LANES * t, LANES * (t + 1))
            f = [pops_ref[step - 1, i, :, sl].astype(jnp.float32) * W32[i] for i in range(19)]
            _, u = _velocity(f)
            for a in range(3):
                u_ref[3 * n + a, :, sl] = u[a]
    fields = {19 + k: (lambda rs, ls, k=k: u_ref[k, rs, ls]) for k in range(nu)}
    _put_fields(fields, x_lo, x_hi, y_lo, y_hi, rows, flat)


def _put_fields(fields, x_lo, x_hi, y_lo, y_hi, rows, flat):
    yw = DEPTH * NZ
    for k, get in fields.items():
        x_lo[DEPTH * k : DEPTH * (k + 1), :] = get(slice(0, DEPTH), slice(0, flat))
        x_hi[DEPTH * k : DEPTH * (k + 1), :] = get(slice(rows - DEPTH, rows), slice(0, flat))
        y_lo[k] = get(slice(0, rows), slice(0, yw))
        y_hi[k] = get(slice(0, rows), slice(flat - yw, flat))


def _messages(saved_pops, seed, solid, mask, field):
    steps = saved_pops.shape[0]
    _, rows, flat = seed.shape
    nfield = 19 + 3 * (steps - 1) + 2
    yw = DEPTH * NZ
    shapes = [(nfield * DEPTH, flat), (nfield * DEPTH, flat), (nfield, rows, yw), (nfield, rows, yw)]
    args = [saved_pops, seed, solid, mask, field]

    def full(shape):
        nd = len(shape)
        return pl.BlockSpec(shape, lambda i, _n=nd: (0,) * _n)

    return pl.pallas_call(
        _prep_kernel,
        grid=(1,),
        in_specs=[pl.BlockSpec(memory_space=pl.ANY)] + [full(a.shape) for a in args[1:]],
        out_specs=[full(sh) for sh in shapes],
        out_shape=[jax.ShapeDtypeStruct(sh, jnp.float32) for sh in shapes],
        scratch_shapes=[
            pltpu.VMEM((3 * (steps - 1), rows, flat), jnp.float32),
            pltpu.VMEM((steps - 1,) + saved_pops.shape[1:], saved_pops.dtype),
            pltpu.SemaphoreType.DMA((steps - 1,)),
        ],
    )(*args)


def _shift(n, d):
    return [(i, (i + d) % n) for i in range(n)]


def body(saved_pops, seed_adjoint, solid_label, design_mask, design_field):
    nx = lax.axis_size("gx")
    ny = lax.axis_size("gy")
    _, rows, flat = seed_adjoint.shape
    yw = DEPTH * NZ
    lo_l, hi_l = slice(0, yw), slice(flat - yw, flat)
    x_lo, x_hi, y_lo, y_hi = _messages(saved_pops, seed_adjoint, solid_label, design_mask, design_field)
    hxp = lax.ppermute(x_lo, "gx", _shift(nx, -1))
    hxm = lax.ppermute(x_hi, "gx", _shift(nx, 1))
    hyp = lax.ppermute(y_lo, "gy", _shift(ny, -1))
    hym = lax.ppermute(y_hi, "gy", _shift(ny, 1))
    nfield = y_lo.shape[0]
    xp3 = hxp.reshape(nfield, DEPTH, flat)
    xm3 = hxm.reshape(nfield, DEPTH, flat)
    c_lo = jnp.concatenate([xp3[:, :, lo_l], xm3[:, :, lo_l]], axis=1).reshape(-1, yw)
    c_hi = jnp.concatenate([xp3[:, :, hi_l], xm3[:, :, hi_l]], axis=1).reshape(-1, yw)
    cp = lax.ppermute(c_lo, "gy", _shift(ny, -1))
    cm = lax.ppermute(c_hi, "gy", _shift(ny, 1))
    erows = rows + 2 * DEPTH
    eflat = flat + 2 * yw
    ext = (19, erows, eflat)
    args = [saved_pops, seed_adjoint, solid_label, design_mask, design_field, hxp, hxm, hyp, hym, cp, cm]

    def full(shape):
        nd = len(shape)
        return pl.BlockSpec(shape, lambda i, _n=nd: (0,) * _n)

    adjoint, sensitivity = pl.pallas_call(
        _fused_kernel,
        grid=(1,),
        in_specs=[full(a.shape) for a in args],
        out_specs=[full(seed_adjoint.shape), full((rows, flat))],
        out_shape=[
            jax.ShapeDtypeStruct(seed_adjoint.shape, jnp.float32),
            jax.ShapeDtypeStruct((rows, flat), jnp.float32),
        ],
        scratch_shapes=[
            pltpu.VMEM(ext, jnp.float32),
            pltpu.VMEM(ext, jnp.float32),
            pltpu.VMEM((3, erows, eflat), jnp.float32),
            pltpu.VMEM((erows, eflat), jnp.float32),
            pltpu.VMEM((erows, eflat), jnp.float32),
        ],
    )(*args)
    return (adjoint, sensitivity)


def solution(mesh):
    in_specs = (
        P(None, None, "gx", "gy"),
        P(None, "gx", "gy"),
        P("gx", "gy"),
        P("gx", "gy"),
        P("gx", "gy"),
    )
    out_specs = (P(None, "gx", "gy"), P("gx", "gy"))
    return jax.shard_map(body, mesh=mesh, in_specs=in_specs, out_specs=out_specs, check_vma=False)
```
